128 devices in a mesh: section: 16 (over z_lo, x, core), ctx: 8 (over z_hi, y).
Axes of the slice: x: 4, y: 4, z: 4 (z_hi: 2, z_lo: 2; z = z_hi * 2 + z_lo), core: 2. Of those that a mesh axis runs over, the one named last changes fastest.
Arguments:
- sent_fwd: bfloat16 [16, 1024, 4096], P('section', 'ctx'), may hold values from -6 to 6
- sent_grad: bfloat16 [16, 1024, 4096], P('section', 'ctx'), may hold values from -6 to 6
- saved_bwd: bfloat16 [16, 1024, 4096], P('section', 'ctx'), may hold values from -6 to 6
- norm_gain: float32 [16, 4096], P('section'), may hold values from 0.5 to 1.5
- key_proj: bfloat16 [16, 4096, 512], P('section')
- value_proj: bfloat16 [16, 4096, 512], P('section'), may hold values from -0.09375 to 0.09375
- seg_fwd: int32 [1024], replicated, may hold values from 0 to 3, never falling along the last dimension, each value on 1 to 512 neighbouring positions
- seg_bwd: int32 [1024], replicated, may hold values from 0 to 3, never falling along the last dimension, each value on 1 to 512 neighbouring positions
Outputs:
- fwd_out: bfloat16 [16, 1024, 4096], P('section', 'ctx')
- grad_out: bfloat16 [16, 1024, 4096], P('section', 'ctx')
The draws below stay inside these ranges and needn't reach their ends.
Inputs may be any that keep to these rules, and one draw needn't show every extreme that they name: `seg_fwd`: segment ids never fall along the sequence, each segment has 1 to 512 positions and one has exactly 512. `seg_bwd`: segment ids never fall along the sequence, each segment has 1 to 512 positions and one has exactly 512.
All inputs are finite; a program needn't handle non-finite values.
Results may differ from the reference program's by a relative error of at most 0.02.
The reference program's roundings to bfloat16 on the way count: a program that leaves them out, or rounds other values in their place, can miss the bound.
Values may be sent and summed in bfloat16 or wider, within the bound.
No kernel may reach another device: no remote copies, remote signals or barrier semaphores. Data moves between devices by JAX's collectives and lax.ppermute only.
A program may use at most 128 MiB of HBM per device.

```python
import math
import jax
import jax.numpy as jnp
import numpy as np
from jax import lax

D = 4096
HD = 128
KVH = 4
H = 32
KVD = 512
SEQ = 1024
SECTIONS = 16


def draw_key_proj(key, part):
    normal_key = jax.random.fold_in(key, 11)
    entries = jax.random.normal(normal_key, (SECTIONS, D, KVH, HD), jnp.float32) * D ** (-0.5)
    return entries.reshape(SECTIONS, D, KVH * HD).astype(jnp.bfloat16)


def levels(rng, shape, shards, least, top_value):
    level, own = 1.0, jax.random.fold_in(rng, 6)
    for dim, blocks in shards:
        steps = jnp.exp(jax.random.uniform(jax.random.fold_in(own, dim), (blocks,), jnp.float32, least / len(shards), top_value / len(shards)))
        level = level * jnp.repeat(steps, shape[dim] // blocks).reshape([-1 if axis == dim else 1 for axis in range(len(shape))])
    return level


def length_profile(count, total, limit, slope):
    portions = [(1 << 20) // math.isqrt(standing ** slope) + 1 for standing in range(2, count + 1)]
    spare, given = total - limit - (count - 1), [1] * (count - 1)
    while spare > 0:
        candidates = [i for i in range(count - 1) if given[i] < limit]
        whole, remaining = sum([portions[i] for i in candidates]), spare
        for i in candidates:
            addition = min(limit - given[i], max(1, remaining * portions[i] // whole), spare)
            given[i] = given[i] + addition
            spare = spare - addition
    return np.array([limit] + given)


def uneven_parts(rng, number_of, total, limit, lean):
    if number_of == 2:
        one = jax.random.randint(rng, (), max(1, total - limit), min(limit, total - 1) + 1)
        return jnp.stack([one, total - one])
    sizes = jnp.asarray(length_profile(number_of, total, limit, lean), jnp.int32)
    twos = (number_of - 1) // 2
    giver, sink = sizes[1:1 + 2 * twos:2], sizes[2:2 + 2 * twos:2]
    margin = jnp.minimum(giver - 1, limit - sink)
    passed = jax.random.randint(jax.random.fold_in(rng, 1), (twos,), 0, 1 << 20) % (margin + 1)
    sizes = sizes.at[1:1 + 2 * twos:2].set(giver - passed).at[2:2 + 2 * twos:2].set(sink + passed)
    return sizes[jax.random.permutation(jax.random.fold_in(rng, 2), number_of)]


def scatter_about(stream_key, dims, spread, bound, cuts=(), kind=jnp.bfloat16):
    factor_of = levels(stream_key, dims, cuts, -0.22, 0.18) if cuts else 1.0
    array = jax.random.normal(stream_key, dims, jnp.float32) * spread * factor_of
    return jnp.minimum(jnp.maximum(array, -bound), bound).astype(kind)


def setup_inputs(seed: int = 0) -> dict:
    key_of = jax.random.split(jax.random.key(seed), 9)
    return {
        "sent_fwd": scatter_about(key_of[0], (SECTIONS, SEQ, D), 1.0, 6.0, ((0, 16), (1, 8))),
        "sent_grad": scatter_about(key_of[1], (SECTIONS, SEQ, D), 1.0, 6.0, ((0, 16), (1, 8))),
        "saved_bwd": scatter_about(key_of[2], (SECTIONS, SEQ, D), 1.0, 6.0, ((0, 16), (1, 8))),
        "norm_gain": jnp.clip(1.0 + 0.1 * jax.random.normal(key_of[3], (SECTIONS, D), jnp.float32), 0.5, 1.5),
        "key_proj": draw_key_proj(jax.random.fold_in(key_of[8], 71), 0),
        "value_proj": scatter_about(key_of[5], (SECTIONS, D, KVD), D ** -0.5, 0.09375, ((0, 16),)),
        "seg_fwd": jnp.searchsorted(jnp.cumsum(uneven_parts(key_of[6], 4, SEQ, SEQ // 2, 2)), jnp.arange(SEQ), side="right").astype(jnp.int32),
        "seg_bwd": jnp.searchsorted(jnp.cumsum(uneven_parts(key_of[7], 4, SEQ, SEQ // 2, 2)), jnp.arange(SEQ), side="right").astype(jnp.int32),
    }


EPSILON = 1e-05
NEGATIVE = -1e+30

def normalize(inputs, gain):
    wide = inputs.astype(jnp.float32)
    inverse = lax.rsqrt(lax.optimization_barrier(jnp.mean(wide * wide, axis=-1, keepdims=True)) + EPSILON)
    return (wide * inverse * gain, wide, inverse)

def layer_parts(inputs, gain, key_weight, value_weight):
    seq_len = inputs.shape[0]
    normed, wide, inverse = normalize(inputs, gain)
    flat = normed.astype(jnp.bfloat16)
    keys = jnp.dot(flat, key_weight, preferred_element_type=jnp.float32).astype(jnp.bfloat16)
    values = jnp.dot(flat, value_weight, preferred_element_type=jnp.float32).astype(jnp.bfloat16)
    query = flat.reshape(seq_len, H, HD)
    return (query, keys, values, wide, inverse)

def allowed_of(segment):
    seq_len = segment.shape[0]
    position = jnp.arange(seq_len, dtype=jnp.int32)
    return (position[None, :] <= position[:, None]) & (segment[:, None] == segment[None, :])

def group_scores(query, keys, group_idx, allowed):
    group_size = H // KVH
    query_grp = query[:, group_idx * group_size:(group_idx + 1) * group_size].astype(jnp.float32)
    key_grp = keys[:, group_idx * HD:(group_idx + 1) * HD].astype(jnp.float32)
    scores = jnp.einsum('tgd,sd->gts', query_grp, key_grp) * HD ** (-0.5)
    scores = jnp.where(allowed[None], scores, NEGATIVE)
    rowmax = lax.optimization_barrier(jnp.max(scores, axis=-1, keepdims=True))
    expo = jnp.where(allowed[None], jnp.exp(scores - rowmax), 0.0)
    total = lax.optimization_barrier(jnp.sum(expo, axis=-1))
    return (query_grp, key_grp, expo, total)

def section_pass(operands, seg_fwd, seg_bwd):
    inputs, upstream, saved, gain, key_weight, value_weight = operands
    seq_len = inputs.shape[0]
    group_size = H // KVH
    query, keys, values, wide, inverse = layer_parts(inputs, gain, key_weight, value_weight)
    allowed = allowed_of(seg_fwd)
    pieces = []
    for group_idx in range(KVH):
        query_grp, key_grp, expo, total = group_scores(query, keys, group_idx, allowed)
        value_grp = values[:, group_idx * HD:(group_idx + 1) * HD].astype(jnp.float32)
        weights_b = lax.optimization_barrier(expo.astype(jnp.bfloat16)).astype(jnp.float32)
        attended = jnp.einsum('gts,sd->tgd', weights_b, value_grp) / jnp.transpose(total)[:, :, None]
        pieces.append(attended)
    attended = jnp.concatenate(pieces, axis=1).reshape(seq_len, D)
    fwd_out = (inputs.astype(jnp.float32) + attended).astype(jnp.bfloat16)
    query, keys, values, wide, inverse = layer_parts(saved, gain, key_weight, value_weight)
    allowed = allowed_of(seg_bwd)
    grad_heads = upstream.reshape(seq_len, H, HD)
    dquery_parts, dkey_parts, dvalue_parts = ([], [], [])
    for group_idx in range(KVH):
        query_grp, key_grp, expo, total = group_scores(query, keys, group_idx, allowed)
        value_grp = values[:, group_idx * HD:(group_idx + 1) * HD].astype(jnp.float32)
        grad_grp = grad_heads[:, group_idx * group_size:(group_idx + 1) * group_size].astype(jnp.float32)
        probs = expo / total[:, :, None]
        probs_b = lax.optimization_barrier(probs.astype(jnp.bfloat16)).astype(jnp.float32)
        dprob = jnp.einsum('tgd,sd->gts', grad_grp, value_grp)
        delta = lax.optimization_barrier(jnp.sum(probs * dprob, axis=-1, keepdims=True))
        dscore_b = lax.optimization_barrier((probs * (dprob - delta)).astype(jnp.bfloat16)).astype(jnp.float32)
        dquery_parts.append(jnp.einsum('gts,sd->tgd', dscore_b, key_grp) * HD ** (-0.5))
        dkey_parts.append(jnp.einsum('gts,tgd->sd', dscore_b, query_grp) * HD ** (-0.5))
        dvalue_parts.append(jnp.einsum('gts,tgd->sd', probs_b, grad_grp))
    dquery = jnp.concatenate(dquery_parts, axis=1).reshape(seq_len, D)
    dkeys = jnp.concatenate(dkey_parts, axis=1).astype(jnp.bfloat16)
    dvalues = jnp.concatenate(dvalue_parts, axis=1).astype(jnp.bfloat16)
    dnormed = dquery + jnp.dot(dkeys, jnp.transpose(key_weight), preferred_element_type=jnp.float32)
    dnormed = dnormed + jnp.dot(dvalues, jnp.transpose(value_weight), preferred_element_type=jnp.float32)
    scaled = gain * dnormed
    grad_in = inverse * scaled - wide * inverse ** 3 * lax.optimization_barrier(jnp.mean(wide * scaled, axis=-1, keepdims=True))
    grad_out = (upstream.astype(jnp.float32) + grad_in).astype(jnp.bfloat16)
    return (fwd_out, grad_out)

def reference(sent_fwd, sent_grad, saved_bwd, norm_gain, key_proj, value_proj, seg_fwd, seg_bwd):
    arrived = jnp.roll(sent_fwd, 1, axis=0)
    upstream = jnp.roll(sent_grad, -1, axis=0)
    fwd_out, grad_out = lax.map(lambda operands: section_pass(operands, seg_fwd, seg_bwd), (arrived, upstream, saved_bwd, norm_gain, key_proj, value_proj))
    return (fwd_out, grad_out)
```

```python
import jax
import jax.numpy as jnp
from jax import lax
from jax.sharding import PartitionSpec as P

HD = 128


EPSILON = 1e-05
NEGATIVE = -1e30


def shifted(block, axis, distance):
    devices = range(lax.axis_size(axis))
    route = [((i - distance) % len(devices), i) for i in devices]
    return lax.ppermute(block, axis, route)


def gather_earlier(block, axis):
    count = lax.axis_size(axis)
    slots = [block]
    for distance in range(1, count):
        route = [(i, i + distance) for i in range(count - distance)]
        slots.append(lax.ppermute(block, axis, route))
    return slots


def return_earlier(slots, axis):
    count = lax.axis_size(axis)
    received = []
    for distance in range(1, count):
        route = [(i + distance, i) for i in range(count - distance)]
        received.append(lax.ppermute(slots[distance], axis, route))
    return received


def normalize(inputs, gain):
    wide = inputs.astype(jnp.float32)
    inverse = lax.rsqrt(jnp.mean(wide * wide, axis=-1, keepdims=True) + EPSILON)
    return (wide * inverse * gain, wide, inverse)


def body(sent_fwd, sent_grad, saved_bwd, norm_gain, key_proj, value_proj, seg_fwd, seg_bwd):
    tok_rows = sent_fwd.shape[1]
    width = sent_fwd.shape[2]
    kv_width = key_proj.shape[2]
    heads = width // HD
    kv_heads = kv_width // HD
    group_size = heads // kv_heads
    scale_factor = HD ** (-0.5)
    count = lax.axis_size("ctx")
    rank = lax.axis_index("ctx")
    offset = rank * tok_rows
    query_pos = offset + jnp.arange(tok_rows, dtype=jnp.int32)
    gain = norm_gain[0]
    key_weight = key_proj[0]
    value_weight = value_proj[0]
    arrived = shifted(sent_fwd, "section", 1)[0]
    upstream = shifted(sent_grad, "section", -1)[0]

    def layer_parts(inputs):
        normed, wide, inverse = normalize(inputs, gain)
        flat = normed.astype(jnp.bfloat16)
        keys = jnp.dot(flat, key_weight, preferred_element_type=jnp.float32).astype(jnp.bfloat16)
        values = jnp.dot(flat, value_weight, preferred_element_type=jnp.float32).astype(
            jnp.bfloat16
        )
        return (flat.reshape(tok_rows, heads, HD), keys, values, wide, inverse)

    def allowed_of(segment):
        seg_query = lax.dynamic_slice_in_dim(segment, offset, tok_rows)
        pieces = []
        for distance in range(count):
            block = rank - distance
            start = jnp.maximum(block, 0) * tok_rows
            key_pos = start + jnp.arange(tok_rows, dtype=jnp.int32)
            seg_key = lax.dynamic_slice_in_dim(segment, start, tok_rows)
            pieces.append(
                (block >= 0)
                & (key_pos[None, :] <= query_pos[:, None])
                & (seg_query[:, None] == seg_key[None, :])
            )
        return jnp.concatenate(pieces, axis=1)

    bwd_query, bwd_keys, bwd_values, bwd_wide, bwd_inverse = layer_parts(saved_bwd[0])
    bwd_slots = gather_earlier(jnp.concatenate([bwd_keys, bwd_values], axis=1), "ctx")
    fwd_query, fwd_keys, fwd_values, fwd_wide, fwd_inverse = layer_parts(arrived)
    fwd_slots = gather_earlier(jnp.concatenate([fwd_keys, fwd_values], axis=1), "ctx")

    bwd_all = jnp.concatenate(bwd_slots, axis=0)
    bwd_key_all = bwd_all[:, :kv_width]
    bwd_value_all = bwd_all[:, kv_width:]
    allowed = allowed_of(seg_bwd)
    grad_heads = upstream.reshape(tok_rows, heads, HD)
    dquery_parts, dkey_parts, dvalue_parts = ([], [], [])
    for group_idx in range(kv_heads):
        head_slice = slice(group_idx * group_size, (group_idx + 1) * group_size)
        feat_slice = slice(group_idx * HD, (group_idx + 1) * HD)
        query_grp = bwd_query[:, head_slice]
        key_grp = bwd_key_all[:, feat_slice]
        value_grp = bwd_value_all[:, feat_slice]
        grad_grp = grad_heads[:, head_slice]
        scores = (
            jnp.einsum("tgd,sd->gts", query_grp, key_grp, preferred_element_type=jnp.float32)
            * scale_factor
        )
        scores = jnp.where(allowed[None], scores, NEGATIVE)
        rowmax = jnp.max(scores, axis=-1, keepdims=True)
        expo = jnp.where(allowed[None], jnp.exp(scores - rowmax), 0.0)
        total = jnp.sum(expo, axis=-1, keepdims=True)
        probs = expo / total
        dprob = jnp.einsum("tgd,sd->gts", grad_grp, value_grp, preferred_element_type=jnp.float32)
        delta = jnp.sum(probs * dprob, axis=-1, keepdims=True)
        dscore_b = (probs * (dprob - delta)).astype(jnp.bfloat16)
        dquery_parts.append(
            jnp.einsum("gts,sd->tgd", dscore_b, key_grp, preferred_element_type=jnp.float32)
            * scale_factor
        )
        probs_b = probs.astype(jnp.bfloat16)
        dkey_parts.append(
            jnp.einsum("gts,tgd->sd", dscore_b, query_grp, preferred_element_type=jnp.float32)
            * scale_factor
        )
        dvalue_parts.append(
            jnp.einsum("gts,tgd->sd", probs_b, grad_grp, preferred_element_type=jnp.float32)
        )
    dquery = jnp.concatenate(dquery_parts, axis=1).reshape(tok_rows, width)
    dkv_terms = jnp.concatenate(dkey_parts + dvalue_parts, axis=1)
    dkv_slots = [
        dkv_terms[distance * tok_rows:(distance + 1) * tok_rows].astype(jnp.bfloat16)
        for distance in range(count)
    ]
    dkv_sum = dkv_terms[:tok_rows]
    for piece in return_earlier(dkv_slots, "ctx"):
        dkv_sum = dkv_sum + piece.astype(jnp.float32)
    dkv = dkv_sum.astype(jnp.bfloat16)
    dkeys = dkv[:, :kv_width]
    dvalues = dkv[:, kv_width:]

    fwd_all = jnp.concatenate(fwd_slots, axis=0)
    key_piece = fwd_all[:, :kv_width]
    value_piece = fwd_all[:, kv_width:]
    allowed = allowed_of(seg_fwd)
    new_total = []
    new_acc = []
    for forward_group_idx in range(kv_heads):
        forward_head_slice = slice(
            forward_group_idx * group_size, (forward_group_idx + 1) * group_size
        )
        forward_feat_slice = slice(forward_group_idx * HD, (forward_group_idx + 1) * HD)
        forward_scores = (
            jnp.einsum(
                "tgd,sd->gts",
                fwd_query[:, forward_head_slice],
                key_piece[:, forward_feat_slice],
                preferred_element_type=jnp.float32,
            )
            * scale_factor
        )
        forward_scores = jnp.where(allowed[None], forward_scores, NEGATIVE)
        top_max = jnp.max(forward_scores, axis=-1)
        forward_expo = jnp.where(allowed[None], jnp.exp(forward_scores - top_max[:, :, None]), 0.0)
        new_total.append(jnp.sum(forward_expo, axis=-1))
        product = jnp.einsum(
            "gts,sd->gtd",
            forward_expo.astype(jnp.bfloat16),
            value_piece[:, forward_feat_slice],
            preferred_element_type=jnp.float32,
        )
        new_acc.append(product)
    attended = jnp.concatenate(new_acc, axis=0) / jnp.concatenate(new_total, axis=0)[:, :, None]
    attended = jnp.transpose(attended, (1, 0, 2)).reshape(tok_rows, width)
    fwd_out = (arrived.astype(jnp.float32) + attended).astype(jnp.bfloat16)

    dnormed = dquery + jnp.dot(
        dkeys, jnp.transpose(key_weight), preferred_element_type=jnp.float32
    )
    dnormed = dnormed + jnp.dot(
        dvalues,
        jnp.transpose(value_weight),
        preferred_element_type=jnp.float32,
    )
    scaled = gain * dnormed
    grad_in = bwd_inverse * scaled - bwd_wide * bwd_inverse**3 * jnp.mean(
        bwd_wide * scaled, axis=-1, keepdims=True
    )
    grad_out = (upstream.astype(jnp.float32) + grad_in).astype(jnp.bfloat16)
    return (fwd_out[None], grad_out[None])


def solution(mesh):
    placed = (
        P("section", "ctx", None),
        P("section", "ctx", None),
        P("section", "ctx", None),
        P("section", None),
        P("section", None, None),
        P("section", None, None),
        P(),
        P(),
    )
    return jax.shard_map(
        body,
        mesh=mesh,
        in_specs=placed,
        out_specs=(P("section", "ctx", None), P("section", "ctx", None)),
        check_vma=False,
    )
```

```python
import jax
import jax.numpy as jnp
from jax import lax
from jax.sharding import PartitionSpec as P

HD = 128


EPSILON = 1e-05
NEGATIVE = -1e30


def shifted(block, axis, distance):
    devices = range(lax.axis_size(axis))
    route = [((i - distance) % len(devices), i) for i in devices]
    return lax.ppermute(block, axis, route)


def gather_all(block, axis):
    count = lax.axis_size(axis)
    spread = jnp.broadcast_to(block[None], (count,) + block.shape)
    moved = lax.all_to_all(spread, axis, 0, 0)
    return moved.reshape((count * block.shape[0],) + block.shape[1:])


def reduce_all(terms, axis):
    count = lax.axis_size(axis)
    rows = terms.shape[0] // count
    moved = lax.all_to_all(terms.astype(jnp.bfloat16).reshape((count, rows) + terms.shape[1:]), axis, 0, 0)
    return jnp.sum(moved.astype(jnp.float32), axis=0)


def normalize(inputs, gain):
    wide = inputs.astype(jnp.float32)
    inverse = lax.rsqrt(jnp.mean(wide * wide, axis=-1, keepdims=True) + EPSILON)
    return (wide * inverse * gain, wide, inverse)


def body(sent_fwd, sent_grad, saved_bwd, norm_gain, key_proj, value_proj, seg_fwd, seg_bwd):
    tok_rows = sent_fwd.shape[1]
    width = sent_fwd.shape[2]
    kv_width = key_proj.shape[2]
    heads = width // HD
    kv_heads = kv_width // HD
    group_size = heads // kv_heads
    scale_factor = HD ** (-0.5)
    count = lax.axis_size("ctx")
    rank = lax.axis_index("ctx")
    offset = rank * tok_rows
    query_pos = offset + jnp.arange(tok_rows, dtype=jnp.int32)
    gain = norm_gain[0]
    key_weight = key_proj[0]
    value_weight = value_proj[0]
    arrived = shifted(sent_fwd, "section", 1)[0]
    upstream = shifted(sent_grad, "section", -1)[0]

    def layer_parts(inputs):
        normed, wide, inverse = normalize(inputs, gain)
        flat = normed.astype(jnp.bfloat16)
        keys = jnp.dot(flat, key_weight, preferred_element_type=jnp.float32).astype(jnp.bfloat16)
        values = jnp.dot(flat, value_weight, preferred_element_type=jnp.float32).astype(
            jnp.bfloat16
        )
        return (flat.reshape(tok_rows, heads, HD), keys, values, wide, inverse)

    def allowed_of(segment):
        seg_query = lax.dynamic_slice_in_dim(segment, offset, tok_rows)
        key_pos = jnp.arange(segment.shape[0], dtype=jnp.int32)
        return (key_pos[None, :] <= query_pos[:, None]) & (seg_query[:, None] == segment[None, :])

    bwd_query, bwd_keys, bwd_values, bwd_wide, bwd_inverse = layer_parts(saved_bwd[0])
    bwd_all = gather_all(jnp.concatenate([bwd_keys, bwd_values], axis=1), "ctx")
    fwd_query, fwd_keys, fwd_values, fwd_wide, fwd_inverse = layer_parts(arrived)
    fwd_all = gather_all(jnp.concatenate([fwd_keys, fwd_values], axis=1), "ctx")

    bwd_key_all = bwd_all[:, :kv_width]
    bwd_value_all = bwd_all[:, kv_width:]
    allowed = allowed_of(seg_bwd)
    grad_heads = upstream.reshape(tok_rows, heads, HD)
    dquery_parts, dkey_parts, dvalue_parts = ([], [], [])
    for group_idx in range(kv_heads):
        head_slice = slice(group_idx * group_size, (group_idx + 1) * group_size)
        feat_slice = slice(group_idx * HD, (group_idx + 1) * HD)
        query_grp = bwd_query[:, head_slice]
        key_grp = bwd_key_all[:, feat_slice]
        value_grp = bwd_value_all[:, feat_slice]
        grad_grp = grad_heads[:, head_slice]
        scores = (
            jnp.einsum("tgd,sd->gts", query_grp, key_grp, preferred_element_type=jnp.float32)
            * scale_factor
        )
        scores = jnp.where(allowed[None], scores, NEGATIVE)
        rowmax = jnp.max(scores, axis=-1, keepdims=True)
        expo = jnp.where(allowed[None], jnp.exp(scores - rowmax), 0.0)
        total = jnp.sum(expo, axis=-1, keepdims=True)
        probs = expo / total
        dprob = jnp.einsum("tgd,sd->gts", grad_grp, value_grp, preferred_element_type=jnp.float32)
        delta = jnp.sum(probs * dprob, axis=-1, keepdims=True)
        dscore_b = (probs * (dprob - delta)).astype(jnp.bfloat16)
        dquery_parts.append(
            jnp.einsum("gts,sd->tgd", dscore_b, key_grp, preferred_element_type=jnp.float32)
            * scale_factor
        )
        probs_b = probs.astype(jnp.bfloat16)
        dkey_parts.append(
            jnp.einsum("gts,tgd->sd", dscore_b, query_grp, preferred_element_type=jnp.float32)
            * scale_factor
        )
        dvalue_parts.append(
            jnp.einsum("gts,tgd->sd", probs_b, grad_grp, preferred_element_type=jnp.float32)
        )
    dquery = jnp.concatenate(dquery_parts, axis=1).reshape(tok_rows, width)
    dkv_terms = jnp.concatenate(dkey_parts + dvalue_parts, axis=1)
    dkv_sum = reduce_all(dkv_terms, "ctx")
    dkv = dkv_sum.astype(jnp.bfloat16)
    dkeys = dkv[:, :kv_width]
    dvalues = dkv[:, kv_width:]

    key_piece = fwd_all[:, :kv_width]
    value_piece = fwd_all[:, kv_width:]
    allowed = allowed_of(seg_fwd)
    new_total = []
    new_acc = []
    for forward_group_idx in range(kv_heads):
        forward_head_slice = slice(
            forward_group_idx * group_size, (forward_group_idx + 1) * group_size
        )
        forward_feat_slice = slice(forward_group_idx * HD, (forward_group_idx + 1) * HD)
        forward_scores = (
            jnp.einsum(
                "tgd,sd->gts",
                fwd_query[:, forward_head_slice],
                key_piece[:, forward_feat_slice],
                preferred_element_type=jnp.float32,
            )
            * scale_factor
        )
        forward_scores = jnp.where(allowed[None], forward_scores, NEGATIVE)
        top_max = jnp.max(forward_scores, axis=-1)
        forward_expo = jnp.where(allowed[None], jnp.exp(forward_scores - top_max[:, :, None]), 0.0)
        new_total.append(jnp.sum(forward_expo, axis=-1))
        product = jnp.einsum(
            "gts,sd->gtd",
            forward_expo.astype(jnp.bfloat16),
            value_piece[:, forward_feat_slice],
            preferred_element_type=jnp.float32,
        )
        new_acc.append(product)
    attended = jnp.concatenate(new_acc, axis=0) / jnp.concatenate(new_total, axis=0)[:, :, None]
    attended = jnp.transpose(attended, (1, 0, 2)).reshape(tok_rows, width)
    fwd_out = (arrived.astype(jnp.float32) + attended).astype(jnp.bfloat16)

    dnormed = dquery + jnp.dot(
        dkeys, jnp.transpose(key_weight), preferred_element_type=jnp.float32
    )
    dnormed = dnormed + jnp.dot(
        dvalues,
        jnp.transpose(value_weight),
        preferred_element_type=jnp.float32,
    )
    scaled = gain * dnormed
    grad_in = bwd_inverse * scaled - bwd_wide * bwd_inverse**3 * jnp.mean(
        bwd_wide * scaled, axis=-1, keepdims=True
    )
    grad_out = (upstream.astype(jnp.float32) + grad_in).astype(jnp.bfloat16)
    return (fwd_out[None], grad_out[None])


def solution(mesh):
    placed = (
        P("section", "ctx", None),
        P("section", "ctx", None),
        P("section", "ctx", None),
        P("section", None),
        P("section", None, None),
        P("section", None, None),
        P(),
        P(),
    )
    return jax.shard_map(
        body,
        mesh=mesh,
        in_specs=placed,
        out_specs=(P("section", "ctx", None), P("section", "ctx", None)),
        check_vma=False,
    )
```

```python
import functools

import jax
import jax.numpy as jnp
from jax import lax
from jax.sharding import PartitionSpec as P
from jax.experimental import pallas as pl

HD = 128


EPSILON = 1e-05
NEGATIVE = -1e30


def shifted(block, axis, distance):
    devices = range(lax.axis_size(axis))
    route = [((i - distance) % len(devices), i) for i in devices]
    return lax.ppermute(block, axis, route)


def gather_all(block, axis):
    count = lax.axis_size(axis)
    spread = jnp.broadcast_to(block[None], (count,) + block.shape)
    moved = lax.all_to_all(spread, axis, 0, 0)
    return moved.reshape((count * block.shape[0],) + block.shape[1:])


def reduce_all(terms, axis):
    count = lax.axis_size(axis)
    rows = terms.shape[0] // count
    moved = lax.all_to_all(terms.astype(jnp.bfloat16).reshape((count, rows) + terms.shape[1:]), axis, 0, 0)
    return jnp.sum(moved.astype(jnp.float32), axis=0)


def normalize(inputs, gain):
    wide = inputs.astype(jnp.float32)
    inverse = lax.rsqrt(jnp.mean(wide * wide, axis=-1, keepdims=True) + EPSILON)
    return (wide * inverse * gain, wide, inverse)


INTERPRET = False


def forward_kernel(mask_ref, query_ref, key_ref, value_ref, input_ref, out_ref, *, heads, scale):
    allowed = mask_ref[...] != 0
    keys = key_ref[...]
    values = value_ref[...]
    for head in range(heads):
        cols = slice(head * HD, (head + 1) * HD)
        scores = lax.dot_general(
            query_ref[:, cols], keys, (((1,), (1,)), ((), ())), preferred_element_type=jnp.float32
        ) * scale
        scores = jnp.where(allowed, scores, NEGATIVE)
        rowmax = jnp.max(scores, axis=1, keepdims=True)
        expo = jnp.where(allowed, jnp.exp(scores - rowmax), 0.0)
        total = jnp.sum(expo, axis=1, keepdims=True)
        product = jnp.dot(expo.astype(jnp.bfloat16), values, preferred_element_type=jnp.float32)
        out_ref[:, cols] = (input_ref[:, cols].astype(jnp.float32) + product / total).astype(out_ref.dtype)


def backward_kernel(mask_ref, query_ref, key_ref, value_ref, grad_ref, dquery_ref, dkey_ref, dvalue_ref, *, heads, scale):
    allowed = mask_ref[...] != 0
    keys = key_ref[...]
    values = value_ref[...]
    dkey_acc = jnp.zeros(dkey_ref.shape, jnp.float32)
    dvalue_acc = jnp.zeros(dvalue_ref.shape, jnp.float32)
    for head in range(heads):
        cols = slice(head * HD, (head + 1) * HD)
        query = query_ref[:, cols]
        grad = grad_ref[:, cols]
        scores = lax.dot_general(
            query, keys, (((1,), (1,)), ((), ())), preferred_element_type=jnp.float32
        ) * scale
        scores = jnp.where(allowed, scores, NEGATIVE)
        rowmax = jnp.max(scores, axis=1, keepdims=True)
        expo = jnp.where(allowed, jnp.exp(scores - rowmax), 0.0)
        total = jnp.sum(expo, axis=1, keepdims=True)
        probs = expo / total
        dprob = lax.dot_general(
            grad, values, (((1,), (1,)), ((), ())), preferred_element_type=jnp.float32
        )
        delta = jnp.sum(probs * dprob, axis=1, keepdims=True)
        dscore_b = (probs * (dprob - delta)).astype(jnp.bfloat16)
        probs_b = probs.astype(jnp.bfloat16)
        dquery_ref[:, cols] = jnp.dot(dscore_b, keys, preferred_element_type=jnp.float32) * scale
        dkey_acc = dkey_acc + lax.dot_general(
            dscore_b, query, (((0,), (0,)), ((), ())), preferred_element_type=jnp.float32
        )
        dvalue_acc = dvalue_acc + lax.dot_general(
            probs_b, grad, (((0,), (0,)), ((), ())), preferred_element_type=jnp.float32
        )
    dkey_ref[...] = dkey_acc * scale
    dvalue_ref[...] = dvalue_acc


def attention_forward(mask, query, keys, values, inputs, group_size):
    rows, width = query.shape
    seq_len, kv_width = keys.shape
    groups = kv_width // HD
    cols = group_size * HD
    kernel = functools.partial(forward_kernel, heads=group_size, scale=HD ** (-0.5))
    return pl.pallas_call(
        kernel,
        grid=(groups,),
        in_specs=[
            pl.BlockSpec((rows, seq_len), lambda g: (0, 0)),
            pl.BlockSpec((rows, cols), lambda g: (0, g)),
            pl.BlockSpec((seq_len, HD), lambda g: (0, g)),
            pl.BlockSpec((seq_len, HD), lambda g: (0, g)),
            pl.BlockSpec((rows, cols), lambda g: (0, g)),
        ],
        out_specs=pl.BlockSpec((rows, cols), lambda g: (0, g)),
        out_shape=jax.ShapeDtypeStruct((rows, width), jnp.bfloat16),
        interpret=INTERPRET,
    )(mask, query, keys, values, inputs)


def attention_backward(mask, query, keys, values, grad, group_size):
    rows, width = query.shape
    seq_len, kv_width = keys.shape
    groups = kv_width // HD
    cols = group_size * HD
    kernel = functools.partial(backward_kernel, heads=group_size, scale=HD ** (-0.5))
    return pl.pallas_call(
        kernel,
        grid=(groups,),
        in_specs=[
            pl.BlockSpec((rows, seq_len), lambda g: (0, 0)),
            pl.BlockSpec((rows, cols), lambda g: (0, g)),
            pl.BlockSpec((seq_len, HD), lambda g: (0, g)),
            pl.BlockSpec((seq_len, HD), lambda g: (0, g)),
            pl.BlockSpec((rows, cols), lambda g: (0, g)),
        ],
        out_specs=[
            pl.BlockSpec((rows, cols), lambda g: (0, g)),
            pl.BlockSpec((seq_len, HD), lambda g: (0, g)),
            pl.BlockSpec((seq_len, HD), lambda g: (0, g)),
        ],
        out_shape=[
            jax.ShapeDtypeStruct((rows, width), jnp.float32),
            jax.ShapeDtypeStruct((seq_len, kv_width), jnp.float32),
            jax.ShapeDtypeStruct((seq_len, kv_width), jnp.float32),
        ],
        interpret=INTERPRET,
    )(mask, query, keys, values, grad)


def body(sent_fwd, sent_grad, saved_bwd, norm_gain, key_proj, value_proj, seg_fwd, seg_bwd):
    tok_rows = sent_fwd.shape[1]
    width = sent_fwd.shape[2]
    kv_width = key_proj.shape[2]
    heads = width // HD
    kv_heads = kv_width // HD
    group_size = heads // kv_heads
    scale_factor = HD ** (-0.5)
    count = lax.axis_size("ctx")
    rank = lax.axis_index("ctx")
    offset = rank * tok_rows
    query_pos = offset + jnp.arange(tok_rows, dtype=jnp.int32)
    gain = norm_gain[0]
    key_weight = key_proj[0]
    value_weight = value_proj[0]
    arrived = shifted(sent_fwd, "section", 1)[0]
    upstream = shifted(sent_grad, "section", -1)[0]

    def layer_parts(inputs):
        normed, wide, inverse = normalize(inputs, gain)
        flat = normed.astype(jnp.bfloat16)
        keys = jnp.dot(flat, key_weight, preferred_element_type=jnp.float32).astype(jnp.bfloat16)
        values = jnp.dot(flat, value_weight, preferred_element_type=jnp.float32).astype(
            jnp.bfloat16
        )
        return (flat.reshape(tok_rows, heads, HD), keys, values, wide, inverse)

    def allowed_of(segment):
        seg_query = lax.dynamic_slice_in_dim(segment, offset, tok_rows)
        key_pos = jnp.arange(segment.shape[0], dtype=jnp.int32)
        return (key_pos[None, :] <= query_pos[:, None]) & (seg_query[:, None] == segment[None, :])

    bwd_query, bwd_keys, bwd_values, bwd_wide, bwd_inverse = layer_parts(saved_bwd[0])
    bwd_all = gather_all(jnp.concatenate([bwd_keys, bwd_values], axis=1), "ctx")
    fwd_query, fwd_keys, fwd_values, fwd_wide, fwd_inverse = layer_parts(arrived)
    fwd_all = gather_all(jnp.concatenate([fwd_keys, fwd_values], axis=1), "ctx")

    bwd_key_all = bwd_all[:, :kv_width]
    bwd_value_all = bwd_all[:, kv_width:]
    allowed = allowed_of(seg_bwd).astype(jnp.int32)
    dquery, dkey_terms, dvalue_terms = attention_backward(
        allowed, bwd_query.reshape(tok_rows, width), bwd_key_all, bwd_value_all, upstream, group_size
    )
    dkv_terms = jnp.concatenate([dkey_terms, dvalue_terms], axis=1)
    dkv_sum = reduce_all(dkv_terms, "ctx")
    dkv = dkv_sum.astype(jnp.bfloat16)
    dkeys = dkv[:, :kv_width]
    dvalues = dkv[:, kv_width:]

    key_piece = fwd_all[:, :kv_width]
    value_piece = fwd_all[:, kv_width:]
    allowed = allowed_of(seg_fwd).astype(jnp.int32)
    fwd_out = attention_forward(
        allowed, fwd_query.reshape(tok_rows, width), key_piece, value_piece, arrived, group_size
    )

    dnormed = dquery + jnp.dot(
        dkeys, jnp.transpose(key_weight), preferred_element_type=jnp.float32
    )
    dnormed = dnormed + jnp.dot(
        dvalues,
        jnp.transpose(value_weight),
        preferred_element_type=jnp.float32,
    )
    scaled = gain * dnormed
    grad_in = bwd_inverse * scaled - bwd_wide * bwd_inverse**3 * jnp.mean(
        bwd_wide * scaled, axis=-1, keepdims=True
    )
    grad_out = (upstream.astype(jnp.float32) + grad_in).astype(jnp.bfloat16)
    return (fwd_out[None], grad_out[None])


def solution(mesh):
    placed = (
        P("section", "ctx", None),
        P("section", "ctx", None),
        P("section", "ctx", None),
        P("section", None),
        P("section", None, None),
        P("section", None, None),
        P(),
        P(),
    )
    return jax.shard_map(
        body,
        mesh=mesh,
        in_specs=placed,
        out_specs=(P("section", "ctx", None), P("section", "ctx", None)),
        check_vma=False,
    )
```

```python
import functools

import jax
import jax.numpy as jnp
from jax import lax
from jax.sharding import PartitionSpec as P
from jax.experimental import pallas as pl

HD = 128


EPSILON = 1e-05
NEGATIVE = -1e30


def shifted(block, axis, distance):
    devices = range(lax.axis_size(axis))
    route = [((i - distance) % len(devices), i) for i in devices]
    return lax.ppermute(block, axis, route)


def gather_all(block, axis):
    count = lax.axis_size(axis)
    spread = jnp.broadcast_to(block[None], (count,) + block.shape)
    moved = lax.all_to_all(spread, axis, 0, 0)
    return moved.reshape((count * block.shape[0],) + block.shape[1:])


def reduce_all(terms, axis):
    count = lax.axis_size(axis)
    rows = terms.shape[0] // count
    moved = lax.all_to_all(terms.astype(jnp.bfloat16).reshape((count, rows) + terms.shape[1:]), axis, 0, 0)
    return jnp.sum(moved.astype(jnp.float32), axis=0)


def normalize(inputs, gain):
    wide = inputs.astype(jnp.float32)
    inverse = lax.rsqrt(jnp.mean(wide * wide, axis=-1, keepdims=True) + EPSILON)
    return (wide * inverse * gain, wide, inverse)


INTERPRET = False


def forward_kernel(mask_ref, query_ref, key_ref, value_ref, input_ref, out_ref, *, heads, scale):
    allowed = mask_ref[...] != 0
    keys = key_ref[...]
    values = value_ref[...]
    for head in range(heads):
        cols = slice(head * HD, (head + 1) * HD)
        scores = lax.dot_general(
            query_ref[:, cols], keys, (((1,), (1,)), ((), ())), preferred_element_type=jnp.float32
        ) * scale
        scores = jnp.where(allowed, scores, NEGATIVE)
        rowmax = jnp.max(scores, axis=1, keepdims=True)
        expo = jnp.where(allowed, jnp.exp(scores - rowmax), 0.0)
        total = jnp.sum(expo, axis=1, keepdims=True)
        product = jnp.dot(expo.astype(jnp.bfloat16), values, preferred_element_type=jnp.float32)
        out_ref[:, cols] = (input_ref[:, cols].astype(jnp.float32) + product / total).astype(out_ref.dtype)


def backward_kernel(mask_ref, query_ref, key_ref, value_ref, grad_ref, dquery_ref, dkey_ref, dvalue_ref, *, heads, scale):
    allowed = mask_ref[...] != 0
    keys = key_ref[...]
    values = value_ref[...]
    dkey_acc = jnp.zeros(dkey_ref.shape, jnp.float32)
    dvalue_acc = jnp.zeros(dvalue_ref.shape, jnp.float32)
    for head in range(heads):
        cols = slice(head * HD, (head + 1) * HD)
        query = query_ref[:, cols]
        grad = grad_ref[:, cols]
        scores = lax.dot_general(
            query, keys, (((1,), (1,)), ((), ())), preferred_element_type=jnp.float32
        ) * scale
        scores = jnp.where(allowed, scores, NEGATIVE)
        rowmax = jnp.max(scores, axis=1, keepdims=True)
        expo = jnp.where(allowed, jnp.exp(scores - rowmax), 0.0)
        total = jnp.sum(expo, axis=1, keepdims=True)
        probs = expo / total
        dprob = lax.dot_general(
            grad, values, (((1,), (1,)), ((), ())), preferred_element_type=jnp.float32
        )
        delta = jnp.sum(probs * dprob, axis=1, keepdims=True)
        dscore_b = (probs * (dprob - delta)).astype(jnp.bfloat16)
        probs_b = probs.astype(jnp.bfloat16)
        dquery_ref[:, cols] = jnp.dot(dscore_b, keys, preferred_element_type=jnp.float32) * scale
        dkey_acc = dkey_acc + lax.dot_general(
            dscore_b, query, (((0,), (0,)), ((), ())), preferred_element_type=jnp.float32
        )
        dvalue_acc = dvalue_acc + lax.dot_general(
            probs_b, grad, (((0,), (0,)), ((), ())), preferred_element_type=jnp.float32
        )
    dkey_ref[...] = dkey_acc * scale
    dvalue_ref[...] = dvalue_acc


def attention_forward(mask, query, keys, values, inputs, group_size):
    rows, width = query.shape
    seq_len, kv_width = keys.shape
    groups = kv_width // HD
    cols = group_size * HD
    kernel = functools.partial(forward_kernel, heads=group_size, scale=HD ** (-0.5))
    return pl.pallas_call(
        kernel,
        grid=(groups,),
        in_specs=[
            pl.BlockSpec((rows, seq_len), lambda g: (0, 0)),
            pl.BlockSpec((rows, cols), lambda g: (0, g)),
            pl.BlockSpec((seq_len, HD), lambda g: (0, g)),
            pl.BlockSpec((seq_len, HD), lambda g: (0, g)),
            pl.BlockSpec((rows, cols), lambda g: (0, g)),
        ],
        out_specs=pl.BlockSpec((rows, cols), lambda g: (0, g)),
        out_shape=jax.ShapeDtypeStruct((rows, width), jnp.bfloat16),
        interpret=INTERPRET,
    )(mask, query, keys, values, inputs)


def attention_backward(mask, query, keys, values, grad, group_size):
    rows, width = query.shape
    seq_len, kv_width = keys.shape
    groups = kv_width // HD
    cols = group_size * HD
    kernel = functools.partial(backward_kernel, heads=group_size, scale=HD ** (-0.5))
    return pl.pallas_call(
        kernel,
        grid=(groups,),
        in_specs=[
            pl.BlockSpec((rows, seq_len), lambda g: (0, 0)),
            pl.BlockSpec((rows, cols), lambda g: (0, g)),
            pl.BlockSpec((seq_len, HD), lambda g: (0, g)),
            pl.BlockSpec((seq_len, HD), lambda g: (0, g)),
            pl.BlockSpec((rows, cols), lambda g: (0, g)),
        ],
        out_specs=[
            pl.BlockSpec((rows, cols), lambda g: (0, g)),
            pl.BlockSpec((seq_len, HD), lambda g: (0, g)),
            pl.BlockSpec((seq_len, HD), lambda g: (0, g)),
        ],
        out_shape=[
            jax.ShapeDtypeStruct((rows, width), jnp.float32),
            jax.ShapeDtypeStruct((seq_len, kv_width), jnp.float32),
            jax.ShapeDtypeStruct((seq_len, kv_width), jnp.float32),
        ],
        interpret=INTERPRET,
    )(mask, query, keys, values, grad)


def body(sent_fwd, sent_grad, saved_bwd, norm_gain, key_proj, value_proj, seg_fwd, seg_bwd):
    tok_rows = sent_fwd.shape[1]
    width = sent_fwd.shape[2]
    kv_width = key_proj.shape[2]
    heads = width // HD
    kv_heads = kv_width // HD
    group_size = heads // kv_heads
    scale_factor = HD ** (-0.5)
    count = lax.axis_size("ctx")
    rank = lax.axis_index("ctx")
    offset = rank * tok_rows
    query_pos = offset + jnp.arange(tok_rows, dtype=jnp.int32)
    gain = norm_gain[0]
    key_weight = key_proj[0]
    value_weight = value_proj[0]
    arrived = shifted(sent_fwd, "section", 1)[0]
    upstream = shifted(sent_grad, "section", -1)[0]

    def layer_parts(inputs):
        normed, wide, inverse = normalize(inputs, gain)
        flat = normed.astype(jnp.bfloat16)
        keys = jnp.dot(flat, key_weight, preferred_element_type=jnp.float32).astype(jnp.bfloat16)
        values = jnp.dot(flat, value_weight, preferred_element_type=jnp.float32).astype(
            jnp.bfloat16
        )
        return (flat.reshape(tok_rows, heads, HD), keys, values, wide, inverse)

    def allowed_of(segment):
        seg_query = lax.dynamic_slice_in_dim(segment, offset, tok_rows)
        key_pos = jnp.arange(segment.shape[0], dtype=jnp.int32)
        return (key_pos[None, :] <= query_pos[:, None]) & (seg_query[:, None] == segment[None, :])

    bwd_query, bwd_keys, bwd_values, bwd_wide, bwd_inverse = layer_parts(saved_bwd[0])
    bwd_all = gather_all(jnp.concatenate([bwd_keys, bwd_values], axis=1), "ctx")
    fwd_query, fwd_keys, fwd_values, fwd_wide, fwd_inverse = layer_parts(arrived)
    fwd_kv, bwd_all = lax.optimization_barrier((jnp.concatenate([fwd_keys, fwd_values], axis=1), bwd_all))
    fwd_all = lax.all_gather(fwd_kv, "ctx", axis=0, tiled=True)

    bwd_key_all = bwd_all[:, :kv_width]
    bwd_value_all = bwd_all[:, kv_width:]
    allowed = allowed_of(seg_bwd).astype(jnp.int32)
    dquery, dkey_terms, dvalue_terms = attention_backward(
        allowed, bwd_query.reshape(tok_rows, width), bwd_key_all, bwd_value_all, upstream, group_size
    )
    dkv_terms = jnp.concatenate([dkey_terms, dvalue_terms], axis=1)
    dkv_sum = reduce_all(dkv_terms, "ctx")
    dkv = dkv_sum.astype(jnp.bfloat16)
    dkeys = dkv[:, :kv_width]
    dvalues = dkv[:, kv_width:]

    key_piece = fwd_all[:, :kv_width]
    value_piece = fwd_all[:, kv_width:]
    allowed = allowed_of(seg_fwd).astype(jnp.int32)
    fwd_out = attention_forward(
        allowed, fwd_query.reshape(tok_rows, width), key_piece, value_piece, arrived, group_size
    )

    dnormed = dquery + jnp.dot(
        dkeys, jnp.transpose(key_weight), preferred_element_type=jnp.float32
    )
    dnormed = dnormed + jnp.dot(
        dvalues,
        jnp.transpose(value_weight),
        preferred_element_type=jnp.float32,
    )
    scaled = gain * dnormed
    grad_in = bwd_inverse * scaled - bwd_wide * bwd_inverse**3 * jnp.mean(
        bwd_wide * scaled, axis=-1, keepdims=True
    )
    grad_out = (upstream.astype(jnp.float32) + grad_in).astype(jnp.bfloat16)
    return (fwd_out[None], grad_out[None])


def solution(mesh):
    placed = (
        P("section", "ctx", None),
        P("section", "ctx", None),
        P("section", "ctx", None),
        P("section", None),
        P("section", None, None),
        P("section", None, None),
        P(),
        P(),
    )
    return jax.shard_map(
        body,
        mesh=mesh,
        in_specs=placed,
        out_specs=(P("section", "ctx", None), P("section", "ctx", None)),
        check_vma=False,
    )
```

```python
import functools

import jax
import jax.numpy as jnp
from jax import lax
from jax.sharding import PartitionSpec as P
from jax.experimental import pallas as pl

HD = 128


EPSILON = 1e-05
NEGATIVE = -1e30


def shifted(block, axis, distance):
    devices = range(lax.axis_size(axis))
    route = [((i - distance) % len(devices), i) for i in devices]
    return lax.ppermute(block, axis, route)


def gather_all(block, axis):
    count = lax.axis_size(axis)
    spread = jnp.broadcast_to(block[None], (count,) + block.shape)
    moved = lax.all_to_all(spread, axis, 0, 0)
    return moved.reshape((count * block.shape[0],) + block.shape[1:])


def reduce_earlier(terms, axis):
    count = lax.axis_size(axis)
    rank = lax.axis_index(axis)
    rows = terms.shape[0] // count
    narrow = terms.astype(jnp.bfloat16)
    total = lax.dynamic_slice_in_dim(terms, rank * rows, rows)
    for distance in range(1, count):
        start = jnp.maximum(rank - distance, 0) * rows
        piece = lax.dynamic_slice_in_dim(narrow, start, rows)
        route = [(i + distance, i) for i in range(count - distance)]
        total = total + lax.ppermute(piece, axis, route).astype(jnp.float32)
    return total


def normalize(inputs, gain):
    wide = inputs.astype(jnp.float32)
    inverse = lax.rsqrt(jnp.mean(wide * wide, axis=-1, keepdims=True) + EPSILON)
    return (wide * inverse * gain, wide, inverse)


INTERPRET = False


def forward_kernel(mask_ref, query_ref, key_ref, value_ref, input_ref, out_ref, *, heads, scale):
    allowed = mask_ref[...] != 0
    keys = key_ref[...]
    values = value_ref[...]
    for head in range(heads):
        cols = slice(head * HD, (head + 1) * HD)
        scores = lax.dot_general(
            query_ref[:, cols], keys, (((1,), (1,)), ((), ())), preferred_element_type=jnp.float32
        ) * scale
        scores = jnp.where(allowed, scores, NEGATIVE)
        rowmax = jnp.max(scores, axis=1, keepdims=True)
        expo = jnp.where(allowed, jnp.exp(scores - rowmax), 0.0)
        total = jnp.sum(expo, axis=1, keepdims=True)
        product = jnp.dot(expo.astype(jnp.bfloat16), values, preferred_element_type=jnp.float32)
        out_ref[:, cols] = (input_ref[:, cols].astype(jnp.float32) + product / total).astype(out_ref.dtype)


def backward_kernel(mask_ref, query_ref, key_ref, value_ref, grad_ref, dquery_ref, dkey_ref, dvalue_ref, *, heads, scale):
    allowed = mask_ref[...] != 0
    keys = key_ref[...]
    values = value_ref[...]
    dkey_acc = jnp.zeros(dkey_ref.shape, jnp.float32)
    dvalue_acc = jnp.zeros(dvalue_ref.shape, jnp.float32)
    for head in range(heads):
        cols = slice(head * HD, (head + 1) * HD)
        query = query_ref[:, cols]
        grad = grad_ref[:, cols]
        scores = lax.dot_general(
            query, keys, (((1,), (1,)), ((), ())), preferred_element_type=jnp.float32
        ) * scale
        scores = jnp.where(allowed, scores, NEGATIVE)
        rowmax = jnp.max(scores, axis=1, keepdims=True)
        expo = jnp.where(allowed, jnp.exp(scores - rowmax), 0.0)
        total = jnp.sum(expo, axis=1, keepdims=True)
        probs = expo / total
        dprob = lax.dot_general(
            grad, values, (((1,), (1,)), ((), ())), preferred_element_type=jnp.float32
        )
        delta = jnp.sum(probs * dprob, axis=1, keepdims=True)
        dscore_b = (probs * (dprob - delta)).astype(jnp.bfloat16)
        probs_b = probs.astype(jnp.bfloat16)
        dquery_ref[:, cols] = jnp.dot(dscore_b, keys, preferred_element_type=jnp.float32) * scale
        dkey_acc = dkey_acc + lax.dot_general(
            dscore_b, query, (((0,), (0,)), ((), ())), preferred_element_type=jnp.float32
        )
        dvalue_acc = dvalue_acc + lax.dot_general(
            probs_b, grad, (((0,), (0,)), ((), ())), preferred_element_type=jnp.float32
        )
    dkey_ref[...] = dkey_acc * scale
    dvalue_ref[...] = dvalue_acc


def attention_forward(mask, query, keys, values, inputs, group_size):
    rows, width = query.shape
    seq_len, kv_width = keys.shape
    groups = kv_width // HD
    cols = group_size * HD
    kernel = functools.partial(forward_kernel, heads=group_size, scale=HD ** (-0.5))
    return pl.pallas_call(
        kernel,
        grid=(groups,),
        in_specs=[
            pl.BlockSpec((rows, seq_len), lambda g: (0, 0)),
            pl.BlockSpec((rows, cols), lambda g: (0, g)),
            pl.BlockSpec((seq_len, HD), lambda g: (0, g)),
            pl.BlockSpec((seq_len, HD), lambda g: (0, g)),
            pl.BlockSpec((rows, cols), lambda g: (0, g)),
        ],
        out_specs=pl.BlockSpec((rows, cols), lambda g: (0, g)),
        out_shape=jax.ShapeDtypeStruct((rows, width), jnp.bfloat16),
        interpret=INTERPRET,
    )(mask, query, keys, values, inputs)


def attention_backward(mask, query, keys, values, grad, group_size):
    rows, width = query.shape
    seq_len, kv_width = keys.shape
    groups = kv_width // HD
    cols = group_size * HD
    kernel = functools.partial(backward_kernel, heads=group_size, scale=HD ** (-0.5))
    return pl.pallas_call(
        kernel,
        grid=(groups,),
        in_specs=[
            pl.BlockSpec((rows, seq_len), lambda g: (0, 0)),
            pl.BlockSpec((rows, cols), lambda g: (0, g)),
            pl.BlockSpec((seq_len, HD), lambda g: (0, g)),
            pl.BlockSpec((seq_len, HD), lambda g: (0, g)),
            pl.BlockSpec((rows, cols), lambda g: (0, g)),
        ],
        out_specs=[
            pl.BlockSpec((rows, cols), lambda g: (0, g)),
            pl.BlockSpec((seq_len, HD), lambda g: (0, g)),
            pl.BlockSpec((seq_len, HD), lambda g: (0, g)),
        ],
        out_shape=[
            jax.ShapeDtypeStruct((rows, width), jnp.float32),
            jax.ShapeDtypeStruct((seq_len, kv_width), jnp.float32),
            jax.ShapeDtypeStruct((seq_len, kv_width), jnp.float32),
        ],
        interpret=INTERPRET,
    )(mask, query, keys, values, grad)


def body(sent_fwd, sent_grad, saved_bwd, norm_gain, key_proj, value_proj, seg_fwd, seg_bwd):
    tok_rows = sent_fwd.shape[1]
    width = sent_fwd.shape[2]
    kv_width = key_proj.shape[2]
    heads = width // HD
    kv_heads = kv_width // HD
    group_size = heads // kv_heads
    scale_factor = HD ** (-0.5)
    count = lax.axis_size("ctx")
    rank = lax.axis_index("ctx")
    offset = rank * tok_rows
    query_pos = offset + jnp.arange(tok_rows, dtype=jnp.int32)
    gain = norm_gain[0]
    key_weight = key_proj[0]
    value_weight = value_proj[0]
    arrived = shifted(sent_fwd, "section", 1)[0]
    upstream = shifted(sent_grad, "section", -1)[0]

    def layer_parts(inputs):
        normed, wide, inverse = normalize(inputs, gain)
        flat = normed.astype(jnp.bfloat16)
        keys = jnp.dot(flat, key_weight, preferred_element_type=jnp.float32).astype(jnp.bfloat16)
        values = jnp.dot(flat, value_weight, preferred_element_type=jnp.float32).astype(
            jnp.bfloat16
        )
        return (flat.reshape(tok_rows, heads, HD), keys, values, wide, inverse)

    def allowed_of(segment):
        seg_query = lax.dynamic_slice_in_dim(segment, offset, tok_rows)
        key_pos = jnp.arange(segment.shape[0], dtype=jnp.int32)
        return (key_pos[None, :] <= query_pos[:, None]) & (seg_query[:, None] == segment[None, :])

    bwd_query, bwd_keys, bwd_values, bwd_wide, bwd_inverse = layer_parts(saved_bwd[0])
    bwd_all = gather_all(jnp.concatenate([bwd_keys, bwd_values], axis=1), "ctx")
    fwd_query, fwd_keys, fwd_values, fwd_wide, fwd_inverse = layer_parts(arrived)
    fwd_all = gather_all(jnp.concatenate([fwd_keys, fwd_values], axis=1), "ctx")

    bwd_key_all = bwd_all[:, :kv_width]
    bwd_value_all = bwd_all[:, kv_width:]
    allowed = allowed_of(seg_bwd).astype(jnp.int32)
    dquery, dkey_terms, dvalue_terms = attention_backward(
        allowed, bwd_query.reshape(tok_rows, width), bwd_key_all, bwd_value_all, upstream, group_size
    )
    dkv_terms = jnp.concatenate([dkey_terms, dvalue_terms], axis=1)
    dkv_sum = reduce_earlier(dkv_terms, "ctx")
    dkv = dkv_sum.astype(jnp.bfloat16)
    dkeys = dkv[:, :kv_width]
    dvalues = dkv[:, kv_width:]

    key_piece = fwd_all[:, :kv_width]
    value_piece = fwd_all[:, kv_width:]
    allowed = allowed_of(seg_fwd).astype(jnp.int32)
    fwd_out = attention_forward(
        allowed, fwd_query.reshape(tok_rows, width), key_piece, value_piece, arrived, group_size
    )

    dnormed = dquery + jnp.dot(
        dkeys, jnp.transpose(key_weight), preferred_element_type=jnp.float32
    )
    dnormed = dnormed + jnp.dot(
        dvalues,
        jnp.transpose(value_weight),
        preferred_element_type=jnp.float32,
    )
    scaled = gain * dnormed
    grad_in = bwd_inverse * scaled - bwd_wide * bwd_inverse**3 * jnp.mean(
        bwd_wide * scaled, axis=-1, keepdims=True
    )
    grad_out = (upstream.astype(jnp.float32) + grad_in).astype(jnp.bfloat16)
    return (fwd_out[None], grad_out[None])


def solution(mesh):
    placed = (
        P("section", "ctx", None),
        P("section", "ctx", None),
        P("section", "ctx", None),
        P("section", None),
        P("section", None, None),
        P("section", None, None),
        P(),
        P(),
    )
    return jax.shard_map(
        body,
        mesh=mesh,
        in_specs=placed,
        out_specs=(P("section", "ctx", None), P("section", "ctx", None)),
        check_vma=False,
    )
```

```python
import functools

import jax
import jax.numpy as jnp
from jax import lax
from jax.sharding import PartitionSpec as P
from jax.experimental import pallas as pl

HD = 128


EPSILON = 1e-05
NEGATIVE = -1e30


def shifted(block, axis, distance):
    devices = range(lax.axis_size(axis))
    route = [((i - distance) % len(devices), i) for i in devices]
    return lax.ppermute(block, axis, route)


def gather_two_level(block):
    zh = lax.axis_index("zh")
    partner = lax.ppermute(block, "zh", [(0, 1), (1, 0)])
    pair = jnp.where(zh == 0, jnp.stack([block, partner]), jnp.stack([partner, block]))
    ring = lax.axis_size("y")
    spread = jnp.broadcast_to(pair[None], (ring,) + pair.shape)
    moved = lax.all_to_all(spread, "y", 0, 0)
    return moved.reshape((-1,) + block.shape[1:])


def reduce_two_level(terms, rows):
    zh = lax.axis_index("zh")
    ring = lax.axis_size("y")
    narrow = terms.astype(jnp.bfloat16).reshape((ring, 2, rows) + terms.shape[1:])
    moved = lax.all_to_all(narrow, "y", 0, 0)
    partial = jnp.sum(moved.astype(jnp.float32), axis=0)
    mine = jnp.where(zh == 0, partial[0], partial[1])
    other = jnp.where(zh == 0, partial[1], partial[0])
    got = lax.ppermute(other.astype(jnp.bfloat16), "zh", [(0, 1), (1, 0)])
    return mine + got.astype(jnp.float32)


def normalize(inputs, gain):
    wide = inputs.astype(jnp.float32)
    inverse = lax.rsqrt(jnp.mean(wide * wide, axis=-1, keepdims=True) + EPSILON)
    return (wide * inverse * gain, wide, inverse)


INTERPRET = False


def forward_kernel(mask_ref, query_ref, key_ref, value_ref, input_ref, out_ref, *, heads, scale):
    allowed = mask_ref[...] != 0
    keys = key_ref[...]
    values = value_ref[...]
    for head in range(heads):
        cols = slice(head * HD, (head + 1) * HD)
        scores = lax.dot_general(
            query_ref[:, cols], keys, (((1,), (1,)), ((), ())), preferred_element_type=jnp.float32
        ) * scale
        scores = jnp.where(allowed, scores, NEGATIVE)
        rowmax = jnp.max(scores, axis=1, keepdims=True)
        expo = jnp.where(allowed, jnp.exp(scores - rowmax), 0.0)
        total = jnp.sum(expo, axis=1, keepdims=True)
        product = jnp.dot(expo.astype(jnp.bfloat16), values, preferred_element_type=jnp.float32)
        out_ref[:, cols] = (input_ref[:, cols].astype(jnp.float32) + product / total).astype(out_ref.dtype)


def backward_kernel(mask_ref, query_ref, key_ref, value_ref, grad_ref, dquery_ref, dkey_ref, dvalue_ref, *, heads, scale):
    allowed = mask_ref[...] != 0
    keys = key_ref[...]
    values = value_ref[...]
    dkey_acc = jnp.zeros(dkey_ref.shape, jnp.float32)
    dvalue_acc = jnp.zeros(dvalue_ref.shape, jnp.float32)
    for head in range(heads):
        cols = slice(head * HD, (head + 1) * HD)
        query = query_ref[:, cols]
        grad = grad_ref[:, cols]
        scores = lax.dot_general(
            query, keys, (((1,), (1,)), ((), ())), preferred_element_type=jnp.float32
        ) * scale
        scores = jnp.where(allowed, scores, NEGATIVE)
        rowmax = jnp.max(scores, axis=1, keepdims=True)
        expo = jnp.where(allowed, jnp.exp(scores - rowmax), 0.0)
        total = jnp.sum(expo, axis=1, keepdims=True)
        probs = expo / total
        dprob = lax.dot_general(
            grad, values, (((1,), (1,)), ((), ())), preferred_element_type=jnp.float32
        )
        delta = jnp.sum(probs * dprob, axis=1, keepdims=True)
        dscore_b = (probs * (dprob - delta)).astype(jnp.bfloat16)
        probs_b = probs.astype(jnp.bfloat16)
        dquery_ref[:, cols] = jnp.dot(dscore_b, keys, preferred_element_type=jnp.float32) * scale
        dkey_acc = dkey_acc + lax.dot_general(
            dscore_b, query, (((0,), (0,)), ((), ())), preferred_element_type=jnp.float32
        )
        dvalue_acc = dvalue_acc + lax.dot_general(
            probs_b, grad, (((0,), (0,)), ((), ())), preferred_element_type=jnp.float32
        )
    dkey_ref[...] = dkey_acc * scale
    dvalue_ref[...] = dvalue_acc


def attention_forward(mask, query, keys, values, inputs, group_size):
    rows, width = query.shape
    seq_len, kv_width = keys.shape
    groups = kv_width // HD
    cols = group_size * HD
    kernel = functools.partial(forward_kernel, heads=group_size, scale=HD ** (-0.5))
    return pl.pallas_call(
        kernel,
        grid=(groups,),
        in_specs=[
            pl.BlockSpec((rows, seq_len), lambda g: (0, 0)),
            pl.BlockSpec((rows, cols), lambda g: (0, g)),
            pl.BlockSpec((seq_len, HD), lambda g: (0, g)),
            pl.BlockSpec((seq_len, HD), lambda g: (0, g)),
            pl.BlockSpec((rows, cols), lambda g: (0, g)),
        ],
        out_specs=pl.BlockSpec((rows, cols), lambda g: (0, g)),
        out_shape=jax.ShapeDtypeStruct((rows, width), jnp.bfloat16),
        interpret=INTERPRET,
    )(mask, query, keys, values, inputs)


def attention_backward(mask, query, keys, values, grad, group_size):
    rows, width = query.shape
    seq_len, kv_width = keys.shape
    groups = kv_width // HD
    cols = group_size * HD
    kernel = functools.partial(backward_kernel, heads=group_size, scale=HD ** (-0.5))
    return pl.pallas_call(
        kernel,
        grid=(groups,),
        in_specs=[
            pl.BlockSpec((rows, seq_len), lambda g: (0, 0)),
            pl.BlockSpec((rows, cols), lambda g: (0, g)),
            pl.BlockSpec((seq_len, HD), lambda g: (0, g)),
            pl.BlockSpec((seq_len, HD), lambda g: (0, g)),
            pl.BlockSpec((rows, cols), lambda g: (0, g)),
        ],
        out_specs=[
            pl.BlockSpec((rows, cols), lambda g: (0, g)),
            pl.BlockSpec((seq_len, HD), lambda g: (0, g)),
            pl.BlockSpec((seq_len, HD), lambda g: (0, g)),
        ],
        out_shape=[
            jax.ShapeDtypeStruct((rows, width), jnp.float32),
            jax.ShapeDtypeStruct((seq_len, kv_width), jnp.float32),
            jax.ShapeDtypeStruct((seq_len, kv_width), jnp.float32),
        ],
        interpret=INTERPRET,
    )(mask, query, keys, values, grad)


def body(sent_fwd, sent_grad, saved_bwd, norm_gain, key_proj, value_proj, seg_fwd, seg_bwd):
    tok_rows = sent_fwd.shape[1]
    width = sent_fwd.shape[2]
    kv_width = key_proj.shape[2]
    heads = width // HD
    kv_heads = kv_width // HD
    group_size = heads // kv_heads
    scale_factor = HD ** (-0.5)
    ring = lax.axis_size("y")
    rank = lax.axis_index("zh") * ring + lax.axis_index("y")
    offset = rank * tok_rows
    query_pos = offset + jnp.arange(tok_rows, dtype=jnp.int32)
    gain = norm_gain[0]
    key_weight = key_proj[0]
    value_weight = value_proj[0]
    arrived = shifted(sent_fwd, "section", 1)[0]
    upstream = shifted(sent_grad, "section", -1)[0]

    def layer_parts(inputs):
        normed, wide, inverse = normalize(inputs, gain)
        flat = normed.astype(jnp.bfloat16)
        keys = jnp.dot(flat, key_weight, preferred_element_type=jnp.float32).astype(jnp.bfloat16)
        values = jnp.dot(flat, value_weight, preferred_element_type=jnp.float32).astype(
            jnp.bfloat16
        )
        return (flat.reshape(tok_rows, heads, HD), keys, values, wide, inverse)

    key_pos = (
        (jnp.arange(2, dtype=jnp.int32)[None, :, None] * ring + jnp.arange(ring, dtype=jnp.int32)[:, None, None])
        * tok_rows
        + jnp.arange(tok_rows, dtype=jnp.int32)[None, None, :]
    ).reshape(-1)

    def allowed_of(segment):
        seg_query = lax.dynamic_slice_in_dim(segment, offset, tok_rows)
        seg_key = jnp.transpose(segment.reshape(2, ring, tok_rows), (1, 0, 2)).reshape(-1)
        return (key_pos[None, :] <= query_pos[:, None]) & (seg_query[:, None] == seg_key[None, :])

    bwd_query, bwd_keys, bwd_values, bwd_wide, bwd_inverse = layer_parts(saved_bwd[0])
    bwd_all = gather_two_level(jnp.concatenate([bwd_keys, bwd_values], axis=1))
    fwd_query, fwd_keys, fwd_values, fwd_wide, fwd_inverse = layer_parts(arrived)
    fwd_all = gather_two_level(jnp.concatenate([fwd_keys, fwd_values], axis=1))

    bwd_key_all = bwd_all[:, :kv_width]
    bwd_value_all = bwd_all[:, kv_width:]
    allowed = allowed_of(seg_bwd).astype(jnp.int32)
    dquery, dkey_terms, dvalue_terms = attention_backward(
        allowed, bwd_query.reshape(tok_rows, width), bwd_key_all, bwd_value_all, upstream, group_size
    )
    dkv_terms = jnp.concatenate([dkey_terms, dvalue_terms], axis=1)
    dkv_sum = reduce_two_level(dkv_terms, tok_rows)
    dkv = dkv_sum.astype(jnp.bfloat16)
    dkeys = dkv[:, :kv_width]
    dvalues = dkv[:, kv_width:]

    key_piece = fwd_all[:, :kv_width]
    value_piece = fwd_all[:, kv_width:]
    allowed = allowed_of(seg_fwd).astype(jnp.int32)
    fwd_out = attention_forward(
        allowed, fwd_query.reshape(tok_rows, width), key_piece, value_piece, arrived, group_size
    )

    dnormed = dquery + jnp.dot(
        dkeys, jnp.transpose(key_weight), preferred_element_type=jnp.float32
    )
    dnormed = dnormed + jnp.dot(
        dvalues,
        jnp.transpose(value_weight),
        preferred_element_type=jnp.float32,
    )
    scaled = gain * dnormed
    grad_in = bwd_inverse * scaled - bwd_wide * bwd_inverse**3 * jnp.mean(
        bwd_wide * scaled, axis=-1, keepdims=True
    )
    grad_out = (upstream.astype(jnp.float32) + grad_in).astype(jnp.bfloat16)
    return (fwd_out[None], grad_out[None])


def solution(mesh):
    sections, positions = mesh.devices.shape
    split = jax.sharding.Mesh(
        mesh.devices.reshape(sections, 2, positions // 2), ("section", "zh", "y")
    )
    rows = ("zh", "y")
    placed = (
        P("section", rows, None),
        P("section", rows, None),
        P("section", rows, None),
        P("section", None),
        P("section", None, None),
        P("section", None, None),
        P(),
        P(),
    )
    return jax.shard_map(
        body,
        mesh=split,
        in_specs=placed,
        out_specs=(P("section", rows, None), P("section", rows, None)),
        check_vma=False,
    )
```

```python
import functools

import jax
import jax.numpy as jnp
from jax import lax
from jax.sharding import PartitionSpec as P
from jax.experimental import pallas as pl

HD = 128


EPSILON = 1e-05
NEGATIVE = -1e30


def shifted(block, axis, distance):
    devices = range(lax.axis_size(axis))
    route = [((i - distance) % len(devices), i) for i in devices]
    return lax.ppermute(block, axis, route)


def gather_all(block, axis):
    count = lax.axis_size(axis)
    spread = jnp.broadcast_to(block[None], (count,) + block.shape)
    moved = lax.all_to_all(spread, axis, 0, 0)
    return moved.reshape((count * block.shape[0],) + block.shape[1:])


def reduce_all(terms, axis):
    count = lax.axis_size(axis)
    rows = terms.shape[0] // count
    moved = lax.all_to_all(terms.astype(jnp.bfloat16).reshape((count, rows) + terms.shape[1:]), axis, 0, 0)
    return jnp.sum(moved.astype(jnp.float32), axis=0)


def normalize(inputs, gain):
    wide = inputs.astype(jnp.float32)
    inverse = lax.rsqrt(jnp.mean(wide * wide, axis=-1, keepdims=True) + EPSILON)
    return (wide * inverse * gain, wide, inverse)


INTERPRET = False


def forward_kernel(mask_ref, query_ref, key_ref, value_ref, input_ref, out_ref, *, heads, scale):
    allowed = mask_ref[...] != 0
    keys = key_ref[...]
    values = value_ref[...]
    for head in range(heads):
        cols = slice(head * HD, (head + 1) * HD)
        scores = lax.dot_general(
            query_ref[:, cols], keys, (((1,), (1,)), ((), ())), preferred_element_type=jnp.float32
        ) * scale
        scores = jnp.where(allowed, scores, NEGATIVE)
        rowmax = jnp.max(scores, axis=1, keepdims=True)
        expo = jnp.where(allowed, jnp.exp(scores - rowmax), 0.0)
        total = jnp.sum(expo, axis=1, keepdims=True)
        product = jnp.dot(expo.astype(jnp.bfloat16), values, preferred_element_type=jnp.float32)
        out_ref[:, cols] = (input_ref[:, cols].astype(jnp.float32) + product / total).astype(out_ref.dtype)


def backward_kernel(mask_ref, query_ref, key_ref, value_ref, grad_ref, dquery_ref, dkey_ref, dvalue_ref, *, heads, scale):
    allowed = mask_ref[...] != 0
    keys = key_ref[...]
    values = value_ref[...]
    dkey_acc = jnp.zeros(dkey_ref.shape, jnp.float32)
    dvalue_acc = jnp.zeros(dvalue_ref.shape, jnp.float32)
    for head in range(heads):
        cols = slice(head * HD, (head + 1) * HD)
        query = query_ref[:, cols]
        grad = grad_ref[:, cols]
        scores = lax.dot_general(
            query, keys, (((1,), (1,)), ((), ())), preferred_element_type=jnp.float32
        ) * scale
        scores = jnp.where(allowed, scores, NEGATIVE)
        rowmax = jnp.max(scores, axis=1, keepdims=True)
        expo = jnp.where(allowed, jnp.exp(scores - rowmax), 0.0)
        total = jnp.sum(expo, axis=1, keepdims=True)
        probs = expo / total
        dprob = lax.dot_general(
            grad, values, (((1,), (1,)), ((), ())), preferred_element_type=jnp.float32
        )
        delta = jnp.sum(probs * dprob, axis=1, keepdims=True)
        dscore_b = (probs * (dprob - delta)).astype(jnp.bfloat16)
        probs_b = probs.astype(jnp.bfloat16)
        dquery_ref[:, cols] = jnp.dot(dscore_b, keys, preferred_element_type=jnp.float32) * scale
        dkey_acc = dkey_acc + lax.dot_general(
            dscore_b, query, (((0,), (0,)), ((), ())), preferred_element_type=jnp.float32
        )
        dvalue_acc = dvalue_acc + lax.dot_general(
            probs_b, grad, (((0,), (0,)), ((), ())), preferred_element_type=jnp.float32
        )
    dkey_ref[...] = dkey_acc * scale
    dvalue_ref[...] = dvalue_acc


def attention_forward(mask, query, keys, values, inputs, group_size):
    rows, width = query.shape
    seq_len, kv_width = keys.shape
    groups = kv_width // HD
    cols = group_size * HD
    kernel = functools.partial(forward_kernel, heads=group_size, scale=HD ** (-0.5))
    return pl.pallas_call(
        kernel,
        grid=(groups,),
        in_specs=[
            pl.BlockSpec((rows, seq_len), lambda g: (0, 0)),
            pl.BlockSpec((rows, cols), lambda g: (0, g)),
            pl.BlockSpec((seq_len, HD), lambda g: (0, g)),
            pl.BlockSpec((seq_len, HD), lambda g: (0, g)),
            pl.BlockSpec((rows, cols), lambda g: (0, g)),
        ],
        out_specs=pl.BlockSpec((rows, cols), lambda g: (0, g)),
        out_shape=jax.ShapeDtypeStruct((rows, width), jnp.bfloat16),
        interpret=INTERPRET,
    )(mask, query, keys, values, inputs)


def attention_backward(mask, query, keys, values, grad, group_size):
    rows, width = query.shape
    seq_len, kv_width = keys.shape
    groups = kv_width // HD
    cols = group_size * HD
    kernel = functools.partial(backward_kernel, heads=group_size, scale=HD ** (-0.5))
    return pl.pallas_call(
        kernel,
        grid=(groups,),
        in_specs=[
            pl.BlockSpec((rows, seq_len), lambda g: (0, 0)),
            pl.BlockSpec((rows, cols), lambda g: (0, g)),
            pl.BlockSpec((seq_len, HD), lambda g: (0, g)),
            pl.BlockSpec((seq_len, HD), lambda g: (0, g)),
            pl.BlockSpec((rows, cols), lambda g: (0, g)),
        ],
        out_specs=[
            pl.BlockSpec((rows, cols), lambda g: (0, g)),
            pl.BlockSpec((seq_len, HD), lambda g: (0, g)),
            pl.BlockSpec((seq_len, HD), lambda g: (0, g)),
        ],
        out_shape=[
            jax.ShapeDtypeStruct((rows, width), jnp.float32),
            jax.ShapeDtypeStruct((seq_len, kv_width), jnp.float32),
            jax.ShapeDtypeStruct((seq_len, kv_width), jnp.float32),
        ],
        interpret=INTERPRET,
    )(mask, query, keys, values, grad)


def body(sent_fwd, sent_grad, saved_bwd, norm_gain, key_proj, value_proj, seg_fwd, seg_bwd):
    tok_rows = sent_fwd.shape[1]
    width = sent_fwd.shape[2]
    kv_width = key_proj.shape[2]
    heads = width // HD
    kv_heads = kv_width // HD
    group_size = heads // kv_heads
    scale_factor = HD ** (-0.5)
    count = lax.axis_size("ctx")
    rank = lax.axis_index("ctx")
    offset = rank * tok_rows
    query_pos = offset + jnp.arange(tok_rows, dtype=jnp.int32)
    gain = norm_gain[0]
    key_weight = key_proj[0]
    value_weight = value_proj[0]
    arrived = shifted(sent_fwd, "section", 1)[0]
    upstream = shifted(sent_grad, "section", -1)[0]

    def layer_parts(inputs):
        normed, wide, inverse = normalize(inputs, gain)
        flat = normed.astype(jnp.bfloat16)
        keys = jnp.dot(flat, key_weight, preferred_element_type=jnp.float32).astype(jnp.bfloat16)
        values = jnp.dot(flat, value_weight, preferred_element_type=jnp.float32).astype(
            jnp.bfloat16
        )
        return (flat.reshape(tok_rows, heads, HD), keys, values, wide, inverse)

    def allowed_of(segment):
        seg_query = lax.dynamic_slice_in_dim(segment, offset, tok_rows)
        key_pos = jnp.arange(segment.shape[0], dtype=jnp.int32)
        return (key_pos[None, :] <= query_pos[:, None]) & (seg_query[:, None] == segment[None, :])

    bwd_query, bwd_keys, bwd_values, bwd_wide, bwd_inverse = layer_parts(saved_bwd[0])
    bwd_all = gather_all(jnp.concatenate([bwd_keys, bwd_values], axis=1), "ctx")
    fwd_query, fwd_keys, fwd_values, fwd_wide, fwd_inverse = layer_parts(arrived)
    fwd_all = gather_all(jnp.concatenate([fwd_keys, fwd_values], axis=1), "ctx")

    bwd_key_all = bwd_all[:, :kv_width]
    bwd_value_all = bwd_all[:, kv_width:]
    allowed = allowed_of(seg_bwd).astype(jnp.int32)
    halves = 2
    half_kv = kv_width // halves
    half_q = width // halves
    dquery_parts, dkey_parts, dvalue_parts = ([], [], [])
    for half in range(halves):
        kv_cols = slice(half * half_kv, (half + 1) * half_kv)
        q_cols = slice(half * half_q, (half + 1) * half_q)
        dquery_half, dkey_half, dvalue_half = attention_backward(
            allowed,
            bwd_query.reshape(tok_rows, width)[:, q_cols],
            bwd_key_all[:, kv_cols],
            bwd_value_all[:, kv_cols],
            upstream[:, q_cols],
            group_size,
        )
        if half == 0:
            fwd_all, dkey_half, dvalue_half = lax.optimization_barrier((fwd_all, dkey_half, dvalue_half))
        dkv_half = reduce_all(jnp.concatenate([dkey_half, dvalue_half], axis=1), "ctx").astype(jnp.bfloat16)
        dquery_parts.append(dquery_half)
        dkey_parts.append(dkv_half[:, :half_kv])
        dvalue_parts.append(dkv_half[:, half_kv:])
    dquery = jnp.concatenate(dquery_parts, axis=1)
    dkeys = jnp.concatenate(dkey_parts, axis=1)
    dvalues = jnp.concatenate(dvalue_parts, axis=1)

    key_piece = fwd_all[:, :kv_width]
    value_piece = fwd_all[:, kv_width:]
    allowed = allowed_of(seg_fwd).astype(jnp.int32)
    fwd_parts = []
    for half in range(halves):
        kv_cols = slice(half * half_kv, (half + 1) * half_kv)
        q_cols = slice(half * half_q, (half + 1) * half_q)
        fwd_parts.append(
            attention_forward(
                allowed,
                fwd_query.reshape(tok_rows, width)[:, q_cols],
                key_piece[:, kv_cols],
                value_piece[:, kv_cols],
                arrived[:, q_cols],
                group_size,
            )
        )
    fwd_out = jnp.concatenate(fwd_parts, axis=1)

    dnormed = dquery + jnp.dot(
        dkeys, jnp.transpose(key_weight), preferred_element_type=jnp.float32
    )
    dnormed = dnormed + jnp.dot(
        dvalues,
        jnp.transpose(value_weight),
        preferred_element_type=jnp.float32,
    )
    scaled = gain * dnormed
    grad_in = bwd_inverse * scaled - bwd_wide * bwd_inverse**3 * jnp.mean(
        bwd_wide * scaled, axis=-1, keepdims=True
    )
    grad_out = (upstream.astype(jnp.float32) + grad_in).astype(jnp.bfloat16)
    return (fwd_out[None], grad_out[None])


def solution(mesh):
    placed = (
        P("section", "ctx", None),
        P("section", "ctx", None),
        P("section", "ctx", None),
        P("section", None),
        P("section", None, None),
        P("section", None, None),
        P(),
        P(),
    )
    return jax.shard_map(
        body,
        mesh=mesh,
        in_specs=placed,
        out_specs=(P("section", "ctx", None), P("section", "ctx", None)),
        check_vma=False,
    )
```

```python
import functools

import jax
import jax.numpy as jnp
from jax import lax
from jax.sharding import PartitionSpec as P
from jax.experimental import pallas as pl

HD = 128


EPSILON = 1e-05
NEGATIVE = -1e30


def shifted(block, axis, distance):
    devices = range(lax.axis_size(axis))
    route = [((i - distance) % len(devices), i) for i in devices]
    return lax.ppermute(block, axis, route)


def gather_all(block, axis):
    count = lax.axis_size(axis)
    spread = jnp.broadcast_to(block[None], (count,) + block.shape)
    moved = lax.all_to_all(spread, axis, 0, 0)
    return moved.reshape((count * block.shape[0],) + block.shape[1:])


def reduce_all(terms, axis):
    count = lax.axis_size(axis)
    rows = terms.shape[0] // count
    moved = lax.all_to_all(terms.astype(jnp.bfloat16).reshape((count, rows) + terms.shape[1:]), axis, 0, 0)
    return jnp.sum(moved.astype(jnp.float32), axis=0)


def normalize(inputs, gain):
    wide = inputs.astype(jnp.float32)
    inverse = lax.rsqrt(jnp.mean(wide * wide, axis=-1, keepdims=True) + EPSILON)
    return (wide * inverse * gain, wide, inverse)


INTERPRET = False


def forward_kernel(mask_ref, query_ref, key_ref, value_ref, input_ref, out_ref, *, heads, scale):
    allowed = mask_ref[...] != 0
    keys = key_ref[...]
    values = value_ref[...]
    for head in range(heads):
        cols = slice(head * HD, (head + 1) * HD)
        scores = lax.dot_general(
            query_ref[:, cols], keys, (((1,), (1,)), ((), ())), preferred_element_type=jnp.float32
        ) * scale
        scores = jnp.where(allowed, scores, NEGATIVE)
        rowmax = jnp.max(scores, axis=1, keepdims=True)
        expo = jnp.where(allowed, jnp.exp(scores - rowmax), 0.0)
        total = jnp.sum(expo, axis=1, keepdims=True)
        product = jnp.dot(expo.astype(jnp.bfloat16), values, preferred_element_type=jnp.float32)
        out_ref[:, cols] = (input_ref[:, cols].astype(jnp.float32) + product / total).astype(out_ref.dtype)


def backward_kernel(mask_ref, query_ref, key_ref, value_ref, grad_ref, dquery_ref, dkey_ref, dvalue_ref, *, heads, scale):
    allowed = mask_ref[...] != 0
    keys = key_ref[...]
    values = value_ref[...]
    dkey_acc = jnp.zeros(dkey_ref.shape, jnp.float32)
    dvalue_acc = jnp.zeros(dvalue_ref.shape, jnp.float32)
    for head in range(heads):
        cols = slice(head * HD, (head + 1) * HD)
        query = query_ref[:, cols]
        grad = grad_ref[:, cols]
        scores = lax.dot_general(
            query, keys, (((1,), (1,)), ((), ())), preferred_element_type=jnp.float32
        ) * scale
        scores = jnp.where(allowed, scores, NEGATIVE)
        rowmax = jnp.max(scores, axis=1, keepdims=True)
        expo = jnp.where(allowed, jnp.exp(scores - rowmax), 0.0)
        total = jnp.sum(expo, axis=1, keepdims=True)
        probs = expo / total
        dprob = lax.dot_general(
            grad, values, (((1,), (1,)), ((), ())), preferred_element_type=jnp.float32
        )
        delta = jnp.sum(probs * dprob, axis=1, keepdims=True)
        dscore_b = (probs * (dprob - delta)).astype(jnp.bfloat16)
        probs_b = probs.astype(jnp.bfloat16)
        dquery_ref[:, cols] = jnp.dot(dscore_b, keys, preferred_element_type=jnp.float32) * scale
        dkey_acc = dkey_acc + lax.dot_general(
            dscore_b, query, (((0,), (0,)), ((), ())), preferred_element_type=jnp.float32
        )
        dvalue_acc = dvalue_acc + lax.dot_general(
            probs_b, grad, (((0,), (0,)), ((), ())), preferred_element_type=jnp.float32
        )
    dkey_ref[...] = dkey_acc * scale
    dvalue_ref[...] = dvalue_acc


def attention_forward(mask, query, keys, values, inputs, group_size):
    rows, width = query.shape
    seq_len, kv_width = keys.shape
    groups = kv_width // HD
    cols = group_size * HD
    kernel = functools.partial(forward_kernel, heads=group_size, scale=HD ** (-0.5))
    return pl.pallas_call(
        kernel,
        grid=(groups,),
        in_specs=[
            pl.BlockSpec((rows, seq_len), lambda g: (0, 0)),
            pl.BlockSpec((rows, cols), lambda g: (0, g)),
            pl.BlockSpec((seq_len, HD), lambda g: (0, g)),
            pl.BlockSpec((seq_len, HD), lambda g: (0, g)),
            pl.BlockSpec((rows, cols), lambda g: (0, g)),
        ],
        out_specs=pl.BlockSpec((rows, cols), lambda g: (0, g)),
        out_shape=jax.ShapeDtypeStruct((rows, width), jnp.bfloat16),
        interpret=INTERPRET,
    )(mask, query, keys, values, inputs)


def attention_backward(mask, query, keys, values, grad, group_size):
    rows, width = query.shape
    seq_len, kv_width = keys.shape
    groups = kv_width // HD
    cols = group_size * HD
    kernel = functools.partial(backward_kernel, heads=group_size, scale=HD ** (-0.5))
    return pl.pallas_call(
        kernel,
        grid=(groups,),
        in_specs=[
            pl.BlockSpec((rows, seq_len), lambda g: (0, 0)),
            pl.BlockSpec((rows, cols), lambda g: (0, g)),
            pl.BlockSpec((seq_len, HD), lambda g: (0, g)),
            pl.BlockSpec((seq_len, HD), lambda g: (0, g)),
            pl.BlockSpec((rows, cols), lambda g: (0, g)),
        ],
        out_specs=[
            pl.BlockSpec((rows, cols), lambda g: (0, g)),
            pl.BlockSpec((seq_len, HD), lambda g: (0, g)),
            pl.BlockSpec((seq_len, HD), lambda g: (0, g)),
        ],
        out_shape=[
            jax.ShapeDtypeStruct((rows, width), jnp.float32),
            jax.ShapeDtypeStruct((seq_len, kv_width), jnp.float32),
            jax.ShapeDtypeStruct((seq_len, kv_width), jnp.float32),
        ],
        interpret=INTERPRET,
    )(mask, query, keys, values, grad)


def body(sent_fwd, sent_grad, saved_bwd, norm_gain, key_proj, value_proj, seg_fwd, seg_bwd):
    tok_rows = sent_fwd.shape[1]
    width = sent_fwd.shape[2]
    kv_width = key_proj.shape[2]
    heads = width // HD
    kv_heads = kv_width // HD
    group_size = heads // kv_heads
    scale_factor = HD ** (-0.5)
    count = lax.axis_size("ctx")
    rank = lax.axis_index("ctx")
    offset = rank * tok_rows
    query_pos = offset + jnp.arange(tok_rows, dtype=jnp.int32)
    gain = norm_gain[0]
    key_weight = key_proj[0]
    value_weight = value_proj[0]
    arrived = shifted(sent_fwd, "section", 1)[0]
    upstream = shifted(sent_grad, "section", -1)[0]

    def layer_parts(inputs):
        normed, wide, inverse = normalize(inputs, gain)
        flat = normed.astype(jnp.bfloat16)
        keys = jnp.dot(flat, key_weight, preferred_element_type=jnp.float32).astype(jnp.bfloat16)
        values = jnp.dot(flat, value_weight, preferred_element_type=jnp.float32).astype(
            jnp.bfloat16
        )
        return (flat.reshape(tok_rows, heads, HD), keys, values, wide, inverse)

    def allowed_of(segment):
        seg_query = lax.dynamic_slice_in_dim(segment, offset, tok_rows)
        key_pos = jnp.arange(segment.shape[0], dtype=jnp.int32)
        return (key_pos[None, :] <= query_pos[:, None]) & (seg_query[:, None] == segment[None, :])

    bwd_query, bwd_keys, bwd_values, bwd_wide, bwd_inverse = layer_parts(saved_bwd[0])
    bwd_half_kv = bwd_keys.shape[1] // 2
    bwd_halves = [
        gather_all(
            jnp.concatenate(
                [
                    bwd_keys[:, half * bwd_half_kv:(half + 1) * bwd_half_kv],
                    bwd_values[:, half * bwd_half_kv:(half + 1) * bwd_half_kv],
                ],
                axis=1,
            ),
            "ctx",
        )
        for half in range(2)
    ]
    fwd_query, fwd_keys, fwd_values, fwd_wide, fwd_inverse = layer_parts(arrived)
    fwd_all = gather_all(jnp.concatenate([fwd_keys, fwd_values], axis=1), "ctx")

    allowed = allowed_of(seg_bwd).astype(jnp.int32)
    halves = 2
    half_kv = kv_width // halves
    half_q = width // halves
    dquery_parts, dkey_parts, dvalue_parts = ([], [], [])
    for half in range(halves):
        kv_cols = slice(half * half_kv, (half + 1) * half_kv)
        q_cols = slice(half * half_q, (half + 1) * half_q)
        dquery_half, dkey_half, dvalue_half = attention_backward(
            allowed,
            bwd_query.reshape(tok_rows, width)[:, q_cols],
            bwd_halves[half][:, :half_kv],
            bwd_halves[half][:, half_kv:],
            upstream[:, q_cols],
            group_size,
        )
        if half == 0:
            fwd_all, dkey_half, dvalue_half = lax.optimization_barrier((fwd_all, dkey_half, dvalue_half))
        dkv_half = reduce_all(jnp.concatenate([dkey_half, dvalue_half], axis=1), "ctx").astype(jnp.bfloat16)
        dquery_parts.append(dquery_half)
        dkey_parts.append(dkv_half[:, :half_kv])
        dvalue_parts.append(dkv_half[:, half_kv:])
    dquery = jnp.concatenate(dquery_parts, axis=1)
    dkeys = jnp.concatenate(dkey_parts, axis=1)
    dvalues = jnp.concatenate(dvalue_parts, axis=1)

    key_piece = fwd_all[:, :kv_width]
    value_piece = fwd_all[:, kv_width:]
    allowed = allowed_of(seg_fwd).astype(jnp.int32)
    fwd_parts = []
    for half in range(halves):
        kv_cols = slice(half * half_kv, (half + 1) * half_kv)
        q_cols = slice(half * half_q, (half + 1) * half_q)
        fwd_parts.append(
            attention_forward(
                allowed,
                fwd_query.reshape(tok_rows, width)[:, q_cols],
                key_piece[:, kv_cols],
                value_piece[:, kv_cols],
                arrived[:, q_cols],
                group_size,
            )
        )
    fwd_out = jnp.concatenate(fwd_parts, axis=1)

    dnormed = dquery + jnp.dot(
        dkeys, jnp.transpose(key_weight), preferred_element_type=jnp.float32
    )
    dnormed = dnormed + jnp.dot(
        dvalues,
        jnp.transpose(value_weight),
        preferred_element_type=jnp.float32,
    )
    scaled = gain * dnormed
    grad_in = bwd_inverse * scaled - bwd_wide * bwd_inverse**3 * jnp.mean(
        bwd_wide * scaled, axis=-1, keepdims=True
    )
    grad_out = (upstream.astype(jnp.float32) + grad_in).astype(jnp.bfloat16)
    return (fwd_out[None], grad_out[None])


def solution(mesh):
    placed = (
        P("section", "ctx", None),
        P("section", "ctx", None),
        P("section", "ctx", None),
        P("section", None),
        P("section", None, None),
        P("section", None, None),
        P(),
        P(),
    )
    return jax.shard_map(
        body,
        mesh=mesh,
        in_specs=placed,
        out_specs=(P("section", "ctx", None), P("section", "ctx", None)),
        check_vma=False,
    )
```

```python
import functools

import jax
import jax.numpy as jnp
from jax import lax
from jax.sharding import PartitionSpec as P
from jax.experimental import pallas as pl

HD = 128


EPSILON = 1e-05
NEGATIVE = -1e30


def shifted(block, axis, distance):
    devices = range(lax.axis_size(axis))
    route = [((i - distance) % len(devices), i) for i in devices]
    return lax.ppermute(block, axis, route)


def gather_all(block, axis):
    count = lax.axis_size(axis)
    spread = jnp.broadcast_to(block[None], (count,) + block.shape)
    moved = lax.all_to_all(spread, axis, 0, 0)
    return moved.reshape((count * block.shape[0],) + block.shape[1:])


def reduce_all(terms, axis):
    count = lax.axis_size(axis)
    rows = terms.shape[0] // count
    moved = lax.all_to_all(terms.astype(jnp.bfloat16).reshape((count, rows) + terms.shape[1:]), axis, 0, 0)
    return jnp.sum(moved.astype(jnp.float32), axis=0)


def normalize(inputs, gain):
    wide = inputs.astype(jnp.float32)
    inverse = lax.rsqrt(jnp.mean(wide * wide, axis=-1, keepdims=True) + EPSILON)
    return (wide * inverse * gain, wide, inverse)


INTERPRET = False


def forward_kernel(mask_ref, query_ref, key_ref, value_ref, input_ref, out_ref, *, heads, scale):
    allowed = mask_ref[...] != 0
    keys = key_ref[...]
    values = value_ref[...]
    for head in range(heads):
        cols = slice(head * HD, (head + 1) * HD)
        scores = lax.dot_general(
            query_ref[:, cols], keys, (((1,), (1,)), ((), ())), preferred_element_type=jnp.float32
        ) * scale
        scores = jnp.where(allowed, scores, NEGATIVE)
        rowmax = jnp.max(scores, axis=1, keepdims=True)
        expo = jnp.where(allowed, jnp.exp(scores - rowmax), 0.0)
        total = jnp.sum(expo, axis=1, keepdims=True)
        product = jnp.dot(expo.astype(jnp.bfloat16), values, preferred_element_type=jnp.float32)
        out_ref[:, cols] = (input_ref[:, cols].astype(jnp.float32) + product / total).astype(out_ref.dtype)


def backward_kernel(mask_ref, query_ref, key_ref, value_ref, grad_ref, dquery_ref, dkey_ref, dvalue_ref, *, heads, scale):
    allowed = mask_ref[...] != 0
    keys = key_ref[...]
    values = value_ref[...]
    dkey_acc = jnp.zeros(dkey_ref.shape, jnp.float32)
    dvalue_acc = jnp.zeros(dvalue_ref.shape, jnp.float32)
    for head in range(heads):
        cols = slice(head * HD, (head + 1) * HD)
        query = query_ref[:, cols]
        grad = grad_ref[:, cols]
        scores = lax.dot_general(
            query, keys, (((1,), (1,)), ((), ())), preferred_element_type=jnp.float32
        ) * scale
        scores = jnp.where(allowed, scores, NEGATIVE)
        rowmax = jnp.max(scores, axis=1, keepdims=True)
        expo = jnp.where(allowed, jnp.exp(scores - rowmax), 0.0)
        total = jnp.sum(expo, axis=1, keepdims=True)
        probs = expo / total
        dprob = lax.dot_general(
            grad, values, (((1,), (1,)), ((), ())), preferred_element_type=jnp.float32
        )
        delta = jnp.sum(probs * dprob, axis=1, keepdims=True)
        dscore_b = (probs * (dprob - delta)).astype(jnp.bfloat16)
        probs_b = probs.astype(jnp.bfloat16)
        dquery_ref[:, cols] = jnp.dot(dscore_b, keys, preferred_element_type=jnp.float32) * scale
        dkey_acc = dkey_acc + lax.dot_general(
            dscore_b, query, (((0,), (0,)), ((), ())), preferred_element_type=jnp.float32
        )
        dvalue_acc = dvalue_acc + lax.dot_general(
            probs_b, grad, (((0,), (0,)), ((), ())), preferred_element_type=jnp.float32
        )
    dkey_ref[...] = dkey_acc * scale
    dvalue_ref[...] = dvalue_acc


def attention_forward(mask, query, keys, values, inputs, group_size):
    rows, width = query.shape
    seq_len, kv_width = keys.shape
    groups = kv_width // HD
    cols = group_size * HD
    kernel = functools.partial(forward_kernel, heads=group_size, scale=HD ** (-0.5))
    return pl.pallas_call(
        kernel,
        grid=(groups,),
        in_specs=[
            pl.BlockSpec((rows, seq_len), lambda g: (0, 0)),
            pl.BlockSpec((rows, cols), lambda g: (0, g)),
            pl.BlockSpec((seq_len, HD), lambda g: (0, g)),
            pl.BlockSpec((seq_len, HD), lambda g: (0, g)),
            pl.BlockSpec((rows, cols), lambda g: (0, g)),
        ],
        out_specs=pl.BlockSpec((rows, cols), lambda g: (0, g)),
        out_shape=jax.ShapeDtypeStruct((rows, width), jnp.bfloat16),
        interpret=INTERPRET,
    )(mask, query, keys, values, inputs)


def attention_backward(mask, query, keys, values, grad, group_size):
    rows, width = query.shape
    seq_len, kv_width = keys.shape
    groups = kv_width // HD
    cols = group_size * HD
    kernel = functools.partial(backward_kernel, heads=group_size, scale=HD ** (-0.5))
    return pl.pallas_call(
        kernel,
        grid=(groups,),
        in_specs=[
            pl.BlockSpec((rows, seq_len), lambda g: (0, 0)),
            pl.BlockSpec((rows, cols), lambda g: (0, g)),
            pl.BlockSpec((seq_len, HD), lambda g: (0, g)),
            pl.BlockSpec((seq_len, HD), lambda g: (0, g)),
            pl.BlockSpec((rows, cols), lambda g: (0, g)),
        ],
        out_specs=[
            pl.BlockSpec((rows, cols), lambda g: (0, g)),
            pl.BlockSpec((seq_len, HD), lambda g: (0, g)),
            pl.BlockSpec((seq_len, HD), lambda g: (0, g)),
        ],
        out_shape=[
            jax.ShapeDtypeStruct((rows, width), jnp.float32),
            jax.ShapeDtypeStruct((seq_len, kv_width), jnp.float32),
            jax.ShapeDtypeStruct((seq_len, kv_width), jnp.float32),
        ],
        interpret=INTERPRET,
    )(mask, query, keys, values, grad)


def body(sent_fwd, sent_grad, saved_bwd, norm_gain, key_proj, value_proj, seg_fwd, seg_bwd):
    tok_rows = sent_fwd.shape[1]
    width = sent_fwd.shape[2]
    kv_width = key_proj.shape[2]
    heads = width // HD
    kv_heads = kv_width // HD
    group_size = heads // kv_heads
    scale_factor = HD ** (-0.5)
    count = lax.axis_size("ctx")
    rank = lax.axis_index("ctx")
    offset = rank * tok_rows
    query_pos = offset + jnp.arange(tok_rows, dtype=jnp.int32)
    gain = norm_gain[0]
    key_weight = key_proj[0]
    value_weight = value_proj[0]
    arrived = shifted(sent_fwd, "section", 1)[0]
    upstream = shifted(sent_grad, "section", -1)[0]

    def layer_parts(inputs):
        normed, wide, inverse = normalize(inputs, gain)
        flat = normed.astype(jnp.bfloat16)
        keys = jnp.dot(flat, key_weight, preferred_element_type=jnp.float32).astype(jnp.bfloat16)
        values = jnp.dot(flat, value_weight, preferred_element_type=jnp.float32).astype(
            jnp.bfloat16
        )
        return (flat.reshape(tok_rows, heads, HD), keys, values, wide, inverse)

    def allowed_of(segment):
        seg_query = lax.dynamic_slice_in_dim(segment, offset, tok_rows)
        key_pos = jnp.arange(segment.shape[0], dtype=jnp.int32)
        return (key_pos[None, :] <= query_pos[:, None]) & (seg_query[:, None] == segment[None, :])

    bwd_query, bwd_keys, bwd_values, bwd_wide, bwd_inverse = layer_parts(saved_bwd[0])
    fwd_query, fwd_keys, fwd_values, fwd_wide, fwd_inverse = layer_parts(arrived)
    both_all = gather_all(jnp.concatenate([bwd_keys, bwd_values, fwd_keys, fwd_values], axis=1), "ctx")
    bwd_all = both_all[:, :2 * kv_width]
    fwd_all = both_all[:, 2 * kv_width:]

    bwd_key_all = bwd_all[:, :kv_width]
    bwd_value_all = bwd_all[:, kv_width:]
    allowed = allowed_of(seg_bwd).astype(jnp.int32)
    halves = 2
    half_kv = kv_width // halves
    half_q = width // halves
    dquery_parts, dkey_parts, dvalue_parts = ([], [], [])
    for half in range(halves):
        kv_cols = slice(half * half_kv, (half + 1) * half_kv)
        q_cols = slice(half * half_q, (half + 1) * half_q)
        dquery_half, dkey_half, dvalue_half = attention_backward(
            allowed,
            bwd_query.reshape(tok_rows, width)[:, q_cols],
            bwd_key_all[:, kv_cols],
            bwd_value_all[:, kv_cols],
            upstream[:, q_cols],
            group_size,
        )
        dkv_half = reduce_all(jnp.concatenate([dkey_half, dvalue_half], axis=1), "ctx").astype(jnp.bfloat16)
        dquery_parts.append(dquery_half)
        dkey_parts.append(dkv_half[:, :half_kv])
        dvalue_parts.append(dkv_half[:, half_kv:])
    dquery = jnp.concatenate(dquery_parts, axis=1)
    dkeys = jnp.concatenate(dkey_parts, axis=1)
    dvalues = jnp.concatenate(dvalue_parts, axis=1)

    key_piece = fwd_all[:, :kv_width]
    value_piece = fwd_all[:, kv_width:]
    allowed = allowed_of(seg_fwd).astype(jnp.int32)
    fwd_parts = []
    for half in range(halves):
        kv_cols = slice(half * half_kv, (half + 1) * half_kv)
        q_cols = slice(half * half_q, (half + 1) * half_q)
        fwd_parts.append(
            attention_forward(
                allowed,
                fwd_query.reshape(tok_rows, width)[:, q_cols],
                key_piece[:, kv_cols],
                value_piece[:, kv_cols],
                arrived[:, q_cols],
                group_size,
            )
        )
    fwd_out = jnp.concatenate(fwd_parts, axis=1)

    dnormed = dquery + jnp.dot(
        dkeys, jnp.transpose(key_weight), preferred_element_type=jnp.float32
    )
    dnormed = dnormed + jnp.dot(
        dvalues,
        jnp.transpose(value_weight),
        preferred_element_type=jnp.float32,
    )
    scaled = gain * dnormed
    grad_in = bwd_inverse * scaled - bwd_wide * bwd_inverse**3 * jnp.mean(
        bwd_wide * scaled, axis=-1, keepdims=True
    )
    grad_out = (upstream.astype(jnp.float32) + grad_in).astype(jnp.bfloat16)
    return (fwd_out[None], grad_out[None])


def solution(mesh):
    placed = (
        P("section", "ctx", None),
        P("section", "ctx", None),
        P("section", "ctx", None),
        P("section", None),
        P("section", None, None),
        P("section", None, None),
        P(),
        P(),
    )
    return jax.shard_map(
        body,
        mesh=mesh,
        in_specs=placed,
        out_specs=(P("section", "ctx", None), P("section", "ctx", None)),
        check_vma=False,
    )
```

```python
import functools

import jax
import jax.numpy as jnp
from jax import lax
from jax.sharding import PartitionSpec as P
from jax.experimental import pallas as pl

HD = 128


EPSILON = 1e-05
NEGATIVE = -1e30


def shifted(block, axis, distance):
    devices = range(lax.axis_size(axis))
    route = [((i - distance) % len(devices), i) for i in devices]
    return lax.ppermute(block, axis, route)


def gather_all(block, axis):
    count = lax.axis_size(axis)
    spread = jnp.broadcast_to(block[None], (count,) + block.shape)
    moved = lax.all_to_all(spread, axis, 0, 0)
    return moved.reshape((count * block.shape[0],) + block.shape[1:])


def reduce_all(terms, axis):
    count = lax.axis_size(axis)
    rows = terms.shape[0] // count
    moved = lax.all_to_all(terms.astype(jnp.bfloat16).reshape((count, rows) + terms.shape[1:]), axis, 0, 0)
    return jnp.sum(moved.astype(jnp.float32), axis=0)


def normalize(inputs, gain):
    wide = inputs.astype(jnp.float32)
    inverse = lax.rsqrt(jnp.mean(wide * wide, axis=-1, keepdims=True) + EPSILON)
    return (wide * inverse * gain, wide, inverse)


INTERPRET = False


def forward_kernel(mask_ref, query_ref, key_ref, value_ref, input_ref, out_ref, *, heads, scale):
    allowed = mask_ref[...] != 0
    keys = key_ref[...]
    values = value_ref[...]
    for head in range(heads):
        cols = slice(head * HD, (head + 1) * HD)
        scores = lax.dot_general(
            query_ref[:, cols], keys, (((1,), (1,)), ((), ())), preferred_element_type=jnp.float32
        ) * scale
        scores = jnp.where(allowed, scores, NEGATIVE)
        rowmax = jnp.max(scores, axis=1, keepdims=True)
        expo = jnp.where(allowed, jnp.exp(scores - rowmax), 0.0)
        total = jnp.sum(expo, axis=1, keepdims=True)
        product = jnp.dot(expo.astype(jnp.bfloat16), values, preferred_element_type=jnp.float32)
        out_ref[:, cols] = (input_ref[:, cols].astype(jnp.float32) + product / total).astype(out_ref.dtype)


def backward_kernel(mask_ref, query_ref, key_ref, value_ref, grad_ref, dquery_ref, dkey_ref, dvalue_ref, *, heads, scale):
    allowed = mask_ref[...] != 0
    keys = key_ref[...]
    values = value_ref[...]
    dkey_acc = jnp.zeros(dkey_ref.shape, jnp.float32)
    dvalue_acc = jnp.zeros(dvalue_ref.shape, jnp.float32)
    for head in range(heads):
        cols = slice(head * HD, (head + 1) * HD)
        query = query_ref[:, cols]
        grad = grad_ref[:, cols]
        scores = lax.dot_general(
            query, keys, (((1,), (1,)), ((), ())), preferred_element_type=jnp.float32
        ) * scale
        scores = jnp.where(allowed, scores, NEGATIVE)
        rowmax = jnp.max(scores, axis=1, keepdims=True)
        expo = jnp.where(allowed, jnp.exp(scores - rowmax), 0.0)
        total = jnp.sum(expo, axis=1, keepdims=True)
        probs = expo / total
        dprob = lax.dot_general(
            grad, values, (((1,), (1,)), ((), ())), preferred_element_type=jnp.float32
        )
        delta = jnp.sum(probs * dprob, axis=1, keepdims=True)
        dscore_b = (probs * (dprob - delta)).astype(jnp.bfloat16)
        probs_b = probs.astype(jnp.bfloat16)
        dquery_ref[:, cols] = jnp.dot(dscore_b, keys, preferred_element_type=jnp.float32) * scale
        dkey_acc = dkey_acc + lax.dot_general(
            dscore_b, query, (((0,), (0,)), ((), ())), preferred_element_type=jnp.float32
        )
        dvalue_acc = dvalue_acc + lax.dot_general(
            probs_b, grad, (((0,), (0,)), ((), ())), preferred_element_type=jnp.float32
        )
    dkey_ref[...] = dkey_acc * scale
    dvalue_ref[...] = dvalue_acc


def attention_forward(mask, query, keys, values, inputs, group_size):
    rows, width = query.shape
    seq_len, kv_width = keys.shape
    groups = kv_width // HD
    cols = group_size * HD
    kernel = functools.partial(forward_kernel, heads=group_size, scale=HD ** (-0.5))
    return pl.pallas_call(
        kernel,
        grid=(groups,),
        in_specs=[
            pl.BlockSpec((rows, seq_len), lambda g: (0, 0)),
            pl.BlockSpec((rows, cols), lambda g: (0, g)),
            pl.BlockSpec((seq_len, HD), lambda g: (0, g)),
            pl.BlockSpec((seq_len, HD), lambda g: (0, g)),
            pl.BlockSpec((rows, cols), lambda g: (0, g)),
        ],
        out_specs=pl.BlockSpec((rows, cols), lambda g: (0, g)),
        out_shape=jax.ShapeDtypeStruct((rows, width), jnp.bfloat16),
        interpret=INTERPRET,
    )(mask, query, keys, values, inputs)


def attention_backward(mask, query, keys, values, grad, group_size):
    rows, width = query.shape
    seq_len, kv_width = keys.shape
    groups = kv_width // HD
    cols = group_size * HD
    kernel = functools.partial(backward_kernel, heads=group_size, scale=HD ** (-0.5))
    return pl.pallas_call(
        kernel,
        grid=(groups,),
        in_specs=[
            pl.BlockSpec((rows, seq_len), lambda g: (0, 0)),
            pl.BlockSpec((rows, cols), lambda g: (0, g)),
            pl.BlockSpec((seq_len, HD), lambda g: (0, g)),
            pl.BlockSpec((seq_len, HD), lambda g: (0, g)),
            pl.BlockSpec((rows, cols), lambda g: (0, g)),
        ],
        out_specs=[
            pl.BlockSpec((rows, cols), lambda g: (0, g)),
            pl.BlockSpec((seq_len, HD), lambda g: (0, g)),
            pl.BlockSpec((seq_len, HD), lambda g: (0, g)),
        ],
        out_shape=[
            jax.ShapeDtypeStruct((rows, width), jnp.float32),
            jax.ShapeDtypeStruct((seq_len, kv_width), jnp.float32),
            jax.ShapeDtypeStruct((seq_len, kv_width), jnp.float32),
        ],
        interpret=INTERPRET,
    )(mask, query, keys, values, grad)


def body(sent_fwd, sent_grad, saved_bwd, norm_gain, key_proj, value_proj, seg_fwd, seg_bwd):
    tok_rows = sent_fwd.shape[1]
    width = sent_fwd.shape[2]
    kv_width = key_proj.shape[2]
    heads = width // HD
    kv_heads = kv_width // HD
    group_size = heads // kv_heads
    scale_factor = HD ** (-0.5)
    count = lax.axis_size("ctx")
    rank = lax.axis_index("ctx")
    offset = rank * tok_rows
    query_pos = offset + jnp.arange(tok_rows, dtype=jnp.int32)
    gain = norm_gain[0]
    key_weight = key_proj[0]
    value_weight = value_proj[0]
    arrived = shifted(sent_fwd, "section", 1)[0]
    upstream = shifted(sent_grad, "section", -1)[0]

    def layer_parts(inputs):
        normed, wide, inverse = normalize(inputs, gain)
        flat = normed.astype(jnp.bfloat16)
        keys = jnp.dot(flat, key_weight, preferred_element_type=jnp.float32).astype(jnp.bfloat16)
        values = jnp.dot(flat, value_weight, preferred_element_type=jnp.float32).astype(
            jnp.bfloat16
        )
        return (flat.reshape(tok_rows, heads, HD), keys, values, wide, inverse)

    def allowed_of(segment):
        seg_query = lax.dynamic_slice_in_dim(segment, offset, tok_rows)
        key_pos = jnp.arange(segment.shape[0], dtype=jnp.int32)
        return (key_pos[None, :] <= query_pos[:, None]) & (seg_query[:, None] == segment[None, :])

    bwd_query, bwd_keys, bwd_values, bwd_wide, bwd_inverse = layer_parts(saved_bwd[0])
    bwd_all = gather_all(jnp.concatenate([bwd_keys, bwd_values], axis=1), "ctx")
    fwd_query, fwd_keys, fwd_values, fwd_wide, fwd_inverse = layer_parts(arrived)
    fwd_all = gather_all(jnp.concatenate([fwd_keys, fwd_values], axis=1), "ctx")

    bwd_key_all = bwd_all[:, :kv_width]
    bwd_value_all = bwd_all[:, kv_width:]
    allowed = allowed_of(seg_bwd).astype(jnp.int32)
    halves = 2
    half_kv = kv_width // halves
    half_q = width // halves
    dquery_parts, dkey_parts, dvalue_parts = ([], [], [])
    half_terms = []
    for half in range(halves):
        kv_cols = slice(half * half_kv, (half + 1) * half_kv)
        q_cols = slice(half * half_q, (half + 1) * half_q)
        dquery_half, dkey_half, dvalue_half = attention_backward(
            allowed,
            bwd_query.reshape(tok_rows, width)[:, q_cols],
            bwd_key_all[:, kv_cols],
            bwd_value_all[:, kv_cols],
            upstream[:, q_cols],
            group_size,
        )
        dquery_parts.append(dquery_half)
        half_terms.append(jnp.concatenate([dkey_half, dvalue_half], axis=1))
    fwd_all, half_terms = lax.optimization_barrier((fwd_all, half_terms))
    for terms in half_terms:
        dkv_half = reduce_all(terms, "ctx").astype(jnp.bfloat16)
        dkey_parts.append(dkv_half[:, :half_kv])
        dvalue_parts.append(dkv_half[:, half_kv:])
    dquery = jnp.concatenate(dquery_parts, axis=1)
    dkeys = jnp.concatenate(dkey_parts, axis=1)
    dvalues = jnp.concatenate(dvalue_parts, axis=1)

    key_piece = fwd_all[:, :kv_width]
    value_piece = fwd_all[:, kv_width:]
    allowed = allowed_of(seg_fwd).astype(jnp.int32)
    fwd_parts = []
    for half in range(halves):
        kv_cols = slice(half * half_kv, (half + 1) * half_kv)
        q_cols = slice(half * half_q, (half + 1) * half_q)
        fwd_parts.append(
            attention_forward(
                allowed,
                fwd_query.reshape(tok_rows, width)[:, q_cols],
                key_piece[:, kv_cols],
                value_piece[:, kv_cols],
                arrived[:, q_cols],
                group_size,
            )
        )
    fwd_out = jnp.concatenate(fwd_parts, axis=1)

    dnormed = dquery + jnp.dot(
        dkeys, jnp.transpose(key_weight), preferred_element_type=jnp.float32
    )
    dnormed = dnormed + jnp.dot(
        dvalues,
        jnp.transpose(value_weight),
        preferred_element_type=jnp.float32,
    )
    scaled = gain * dnormed
    grad_in = bwd_inverse * scaled - bwd_wide * bwd_inverse**3 * jnp.mean(
        bwd_wide * scaled, axis=-1, keepdims=True
    )
    grad_out = (upstream.astype(jnp.float32) + grad_in).astype(jnp.bfloat16)
    return (fwd_out[None], grad_out[None])


def solution(mesh):
    placed = (
        P("section", "ctx", None),
        P("section", "ctx", None),
        P("section", "ctx", None),
        P("section", None),
        P("section", None, None),
        P("section", None, None),
        P(),
        P(),
    )
    return jax.shard_map(
        body,
        mesh=mesh,
        in_specs=placed,
        out_specs=(P("section", "ctx", None), P("section", "ctx", None)),
        check_vma=False,
    )
```

```python
import functools

import jax
import jax.numpy as jnp
from jax import lax
from jax.sharding import PartitionSpec as P
from jax.experimental import pallas as pl

HD = 128


EPSILON = 1e-05
NEGATIVE = -1e30
SEGMENT_MAX = 512


def shifted(block, axis, distance):
    devices = range(lax.axis_size(axis))
    route = [((i - distance) % len(devices), i) for i in devices]
    return lax.ppermute(block, axis, route)


def gather_all(block, axis):
    count = lax.axis_size(axis)
    spread = jnp.broadcast_to(block[None], (count,) + block.shape)
    moved = lax.all_to_all(spread, axis, 0, 0)
    return moved.reshape((count * block.shape[0],) + block.shape[1:])


def reduce_all(terms, axis):
    count = lax.axis_size(axis)
    rows = terms.shape[0] // count
    moved = lax.all_to_all(terms.astype(jnp.bfloat16).reshape((count, rows) + terms.shape[1:]), axis, 0, 0)
    return jnp.sum(moved.astype(jnp.float32), axis=0)


def normalize(inputs, gain):
    wide = inputs.astype(jnp.float32)
    inverse = lax.rsqrt(jnp.mean(wide * wide, axis=-1, keepdims=True) + EPSILON)
    return (wide * inverse * gain, wide, inverse)


INTERPRET = False


def forward_kernel(mask_ref, query_ref, key_ref, value_ref, input_ref, out_ref, *, heads, scale):
    allowed = mask_ref[...] != 0
    keys = key_ref[...]
    values = value_ref[...]
    for head in range(heads):
        cols = slice(head * HD, (head + 1) * HD)
        scores = lax.dot_general(
            query_ref[:, cols], keys, (((1,), (1,)), ((), ())), preferred_element_type=jnp.float32
        ) * scale
        scores = jnp.where(allowed, scores, NEGATIVE)
        rowmax = jnp.max(scores, axis=1, keepdims=True)
        expo = jnp.where(allowed, jnp.exp(scores - rowmax), 0.0)
        total = jnp.sum(expo, axis=1, keepdims=True)
        product = jnp.dot(expo.astype(jnp.bfloat16), values, preferred_element_type=jnp.float32)
        out_ref[:, cols] = (input_ref[:, cols].astype(jnp.float32) + product / total).astype(out_ref.dtype)


def backward_kernel(mask_ref, query_ref, key_ref, value_ref, grad_ref, dquery_ref, dkey_ref, dvalue_ref, *, heads, scale):
    allowed = mask_ref[...] != 0
    keys = key_ref[...]
    values = value_ref[...]
    dkey_acc = jnp.zeros(dkey_ref.shape, jnp.float32)
    dvalue_acc = jnp.zeros(dvalue_ref.shape, jnp.float32)
    for head in range(heads):
        cols = slice(head * HD, (head + 1) * HD)
        query = query_ref[:, cols]
        grad = grad_ref[:, cols]
        scores = lax.dot_general(
            query, keys, (((1,), (1,)), ((), ())), preferred_element_type=jnp.float32
        ) * scale
        scores = jnp.where(allowed, scores, NEGATIVE)
        rowmax = jnp.max(scores, axis=1, keepdims=True)
        expo = jnp.where(allowed, jnp.exp(scores - rowmax), 0.0)
        total = jnp.sum(expo, axis=1, keepdims=True)
        probs = expo / total
        dprob = lax.dot_general(
            grad, values, (((1,), (1,)), ((), ())), preferred_element_type=jnp.float32
        )
        delta = jnp.sum(probs * dprob, axis=1, keepdims=True)
        dscore_b = (probs * (dprob - delta)).astype(jnp.bfloat16)
        probs_b = probs.astype(jnp.bfloat16)
        dquery_ref[:, cols] = jnp.dot(dscore_b, keys, preferred_element_type=jnp.float32) * scale
        dkey_acc = dkey_acc + lax.dot_general(
            dscore_b, query, (((0,), (0,)), ((), ())), preferred_element_type=jnp.float32
        )
        dvalue_acc = dvalue_acc + lax.dot_general(
            probs_b, grad, (((0,), (0,)), ((), ())), preferred_element_type=jnp.float32
        )
    dkey_ref[...] = dkey_acc * scale
    dvalue_ref[...] = dvalue_acc


def attention_forward(mask, query, keys, values, inputs, group_size):
    rows, width = query.shape
    seq_len, kv_width = keys.shape
    groups = kv_width // HD
    cols = group_size * HD
    kernel = functools.partial(forward_kernel, heads=group_size, scale=HD ** (-0.5))
    return pl.pallas_call(
        kernel,
        grid=(groups,),
        in_specs=[
            pl.BlockSpec((rows, seq_len), lambda g: (0, 0)),
            pl.BlockSpec((rows, cols), lambda g: (0, g)),
            pl.BlockSpec((seq_len, HD), lambda g: (0, g)),
            pl.BlockSpec((seq_len, HD), lambda g: (0, g)),
            pl.BlockSpec((rows, cols), lambda g: (0, g)),
        ],
        out_specs=pl.BlockSpec((rows, cols), lambda g: (0, g)),
        out_shape=jax.ShapeDtypeStruct((rows, width), jnp.bfloat16),
        interpret=INTERPRET,
    )(mask, query, keys, values, inputs)


def attention_backward(mask, query, keys, values, grad, group_size):
    rows, width = query.shape
    seq_len, kv_width = keys.shape
    groups = kv_width // HD
    cols = group_size * HD
    kernel = functools.partial(backward_kernel, heads=group_size, scale=HD ** (-0.5))
    return pl.pallas_call(
        kernel,
        grid=(groups,),
        in_specs=[
            pl.BlockSpec((rows, seq_len), lambda g: (0, 0)),
            pl.BlockSpec((rows, cols), lambda g: (0, g)),
            pl.BlockSpec((seq_len, HD), lambda g: (0, g)),
            pl.BlockSpec((seq_len, HD), lambda g: (0, g)),
            pl.BlockSpec((rows, cols), lambda g: (0, g)),
        ],
        out_specs=[
            pl.BlockSpec((rows, cols), lambda g: (0, g)),
            pl.BlockSpec((seq_len, HD), lambda g: (0, g)),
            pl.BlockSpec((seq_len, HD), lambda g: (0, g)),
        ],
        out_shape=[
            jax.ShapeDtypeStruct((rows, width), jnp.float32),
            jax.ShapeDtypeStruct((seq_len, kv_width), jnp.float32),
            jax.ShapeDtypeStruct((seq_len, kv_width), jnp.float32),
        ],
        interpret=INTERPRET,
    )(mask, query, keys, values, grad)


def body(sent_fwd, sent_grad, saved_bwd, norm_gain, key_proj, value_proj, seg_fwd, seg_bwd):
    tok_rows = sent_fwd.shape[1]
    width = sent_fwd.shape[2]
    kv_width = key_proj.shape[2]
    heads = width // HD
    kv_heads = kv_width // HD
    group_size = heads // kv_heads
    scale_factor = HD ** (-0.5)
    count = lax.axis_size("ctx")
    rank = lax.axis_index("ctx")
    offset = rank * tok_rows
    query_pos = offset + jnp.arange(tok_rows, dtype=jnp.int32)
    gain = norm_gain[0]
    key_weight = key_proj[0]
    value_weight = value_proj[0]
    arrived = shifted(sent_fwd, "section", 1)[0]
    upstream = shifted(sent_grad, "section", -1)[0]

    def layer_parts(inputs):
        normed, wide, inverse = normalize(inputs, gain)
        flat = normed.astype(jnp.bfloat16)
        keys = jnp.dot(flat, key_weight, preferred_element_type=jnp.float32).astype(jnp.bfloat16)
        values = jnp.dot(flat, value_weight, preferred_element_type=jnp.float32).astype(
            jnp.bfloat16
        )
        return (flat.reshape(tok_rows, heads, HD), keys, values, wide, inverse)

    def allowed_of(segment):
        seg_query = lax.dynamic_slice_in_dim(segment, offset, tok_rows)
        key_pos = jnp.arange(segment.shape[0], dtype=jnp.int32)
        return (key_pos[None, :] <= query_pos[:, None]) & (seg_query[:, None] == segment[None, :])

    back_blocks = -(-(SEGMENT_MAX - 1) // tok_rows)
    window = min(back_blocks + 1, count) * tok_rows
    window_start = jnp.minimum(jnp.maximum(rank - back_blocks, 0) * tok_rows, count * tok_rows - window)

    def windowed(array):
        return lax.dynamic_slice_in_dim(array, window_start, window, axis=0)

    bwd_query, bwd_keys, bwd_values, bwd_wide, bwd_inverse = layer_parts(saved_bwd[0])
    bwd_all = gather_all(jnp.concatenate([bwd_keys, bwd_values], axis=1), "ctx")
    fwd_query, fwd_keys, fwd_values, fwd_wide, fwd_inverse = layer_parts(arrived)
    fwd_all = gather_all(jnp.concatenate([fwd_keys, fwd_values], axis=1), "ctx")

    bwd_key_all = bwd_all[:, :kv_width]
    bwd_value_all = bwd_all[:, kv_width:]
    allowed = lax.dynamic_slice_in_dim(allowed_of(seg_bwd).astype(jnp.int32), window_start, window, axis=1)
    bwd_key_all = windowed(bwd_key_all)
    bwd_value_all = windowed(bwd_value_all)
    halves = 2
    half_kv = kv_width // halves
    half_q = width // halves
    dquery_parts, dkey_parts, dvalue_parts = ([], [], [])
    half_terms = []
    for half in range(halves):
        kv_cols = slice(half * half_kv, (half + 1) * half_kv)
        q_cols = slice(half * half_q, (half + 1) * half_q)
        dquery_half, dkey_half, dvalue_half = attention_backward(
            allowed,
            bwd_query.reshape(tok_rows, width)[:, q_cols],
            bwd_key_all[:, kv_cols],
            bwd_value_all[:, kv_cols],
            upstream[:, q_cols],
            group_size,
        )
        dquery_parts.append(dquery_half)
        terms = jnp.concatenate([dkey_half, dvalue_half], axis=1)
        half_terms.append(
            lax.dynamic_update_slice_in_dim(
                jnp.zeros((count * tok_rows, terms.shape[1]), terms.dtype), terms, window_start, axis=0
            )
        )
    fwd_all, half_terms = lax.optimization_barrier((fwd_all, half_terms))
    for terms in half_terms:
        dkv_half = reduce_all(terms, "ctx").astype(jnp.bfloat16)
        dkey_parts.append(dkv_half[:, :half_kv])
        dvalue_parts.append(dkv_half[:, half_kv:])
    dquery = jnp.concatenate(dquery_parts, axis=1)
    dkeys = jnp.concatenate(dkey_parts, axis=1)
    dvalues = jnp.concatenate(dvalue_parts, axis=1)

    key_piece = windowed(fwd_all[:, :kv_width])
    value_piece = windowed(fwd_all[:, kv_width:])
    allowed = lax.dynamic_slice_in_dim(allowed_of(seg_fwd).astype(jnp.int32), window_start, window, axis=1)
    fwd_parts = []
    for half in range(halves):
        kv_cols = slice(half * half_kv, (half + 1) * half_kv)
        q_cols = slice(half * half_q, (half + 1) * half_q)
        fwd_parts.append(
            attention_forward(
                allowed,
                fwd_query.reshape(tok_rows, width)[:, q_cols],
                key_piece[:, kv_cols],
                value_piece[:, kv_cols],
                arrived[:, q_cols],
                group_size,
            )
        )
    fwd_out = jnp.concatenate(fwd_parts, axis=1)

    dnormed = dquery + jnp.dot(
        dkeys, jnp.transpose(key_weight), preferred_element_type=jnp.float32
    )
    dnormed = dnormed + jnp.dot(
        dvalues,
        jnp.transpose(value_weight),
        preferred_element_type=jnp.float32,
    )
    scaled = gain * dnormed
    grad_in = bwd_inverse * scaled - bwd_wide * bwd_inverse**3 * jnp.mean(
        bwd_wide * scaled, axis=-1, keepdims=True
    )
    grad_out = (upstream.astype(jnp.float32) + grad_in).astype(jnp.bfloat16)
    return (fwd_out[None], grad_out[None])


def solution(mesh):
    placed = (
        P("section", "ctx", None),
        P("section", "ctx", None),
        P("section", "ctx", None),
        P("section", None),
        P("section", None, None),
        P("section", None, None),
        P(),
        P(),
    )
    return jax.shard_map(
        body,
        mesh=mesh,
        in_specs=placed,
        out_specs=(P("section", "ctx", None), P("section", "ctx", None)),
        check_vma=False,
    )
```

```python
import functools

import jax
import jax.numpy as jnp
from jax import lax
from jax.sharding import PartitionSpec as P
from jax.experimental import pallas as pl
from jax.experimental.pallas import tpu as pltpu

HD = 128


EPSILON = 1e-05
NEGATIVE = -1e30
SEGMENT_MAX = 512


def shifted(block, axis, distance):
    devices = range(lax.axis_size(axis))
    route = [((i - distance) % len(devices), i) for i in devices]
    return lax.ppermute(block, axis, route)


def gather_all(block, axis):
    count = lax.axis_size(axis)
    spread = jnp.broadcast_to(block[None], (count,) + block.shape)
    moved = lax.all_to_all(spread, axis, 0, 0)
    return moved.reshape((count * block.shape[0],) + block.shape[1:])


def reduce_all(terms, axis):
    count = lax.axis_size(axis)
    rows = terms.shape[0] // count
    moved = lax.all_to_all(terms.astype(jnp.bfloat16).reshape((count, rows) + terms.shape[1:]), axis, 0, 0)
    return jnp.sum(moved.astype(jnp.float32), axis=0)


def normalize(inputs, gain):
    wide = inputs.astype(jnp.float32)
    inverse = lax.rsqrt(jnp.mean(wide * wide, axis=-1, keepdims=True) + EPSILON)
    return (wide * inverse * gain, wide, inverse)


INTERPRET = False


def forward_kernel(start_ref, mask_ref, query_ref, key_ref, value_ref, input_ref, out_ref, *, heads, scale):
    allowed = mask_ref[...] != 0
    window = mask_ref.shape[1]
    start = pl.multiple_of(start_ref[0], HD)
    keys = key_ref[pl.ds(start, window), :]
    values = value_ref[pl.ds(start, window), :]
    for head in range(heads):
        cols = slice(head * HD, (head + 1) * HD)
        scores = lax.dot_general(
            query_ref[:, cols], keys, (((1,), (1,)), ((), ())), preferred_element_type=jnp.float32
        ) * scale
        scores = jnp.where(allowed, scores, NEGATIVE)
        rowmax = jnp.max(scores, axis=1, keepdims=True)
        expo = jnp.where(allowed, jnp.exp(scores - rowmax), 0.0)
        total = jnp.sum(expo, axis=1, keepdims=True)
        product = jnp.dot(expo.astype(jnp.bfloat16), values, preferred_element_type=jnp.float32)
        out_ref[:, cols] = (input_ref[:, cols].astype(jnp.float32) + product / total).astype(out_ref.dtype)


def backward_kernel(start_ref, mask_ref, query_ref, key_ref, value_ref, grad_ref, dquery_ref, dkey_ref, dvalue_ref, *, heads, scale):
    allowed = mask_ref[...] != 0
    window = mask_ref.shape[1]
    start = pl.multiple_of(start_ref[0], HD)
    keys = key_ref[pl.ds(start, window), :]
    values = value_ref[pl.ds(start, window), :]
    dkey_acc = jnp.zeros((window, HD), jnp.float32)
    dvalue_acc = jnp.zeros((window, HD), jnp.float32)
    for head in range(heads):
        cols = slice(head * HD, (head + 1) * HD)
        query = query_ref[:, cols]
        grad = grad_ref[:, cols]
        scores = lax.dot_general(
            query, keys, (((1,), (1,)), ((), ())), preferred_element_type=jnp.float32
        ) * scale
        scores = jnp.where(allowed, scores, NEGATIVE)
        rowmax = jnp.max(scores, axis=1, keepdims=True)
        expo = jnp.where(allowed, jnp.exp(scores - rowmax), 0.0)
        total = jnp.sum(expo, axis=1, keepdims=True)
        probs = expo / total
        dprob = lax.dot_general(
            grad, values, (((1,), (1,)), ((), ())), preferred_element_type=jnp.float32
        )
        delta = jnp.sum(probs * dprob, axis=1, keepdims=True)
        dscore_b = (probs * (dprob - delta)).astype(jnp.bfloat16)
        probs_b = probs.astype(jnp.bfloat16)
        dquery_ref[:, cols] = jnp.dot(dscore_b, keys, preferred_element_type=jnp.float32) * scale
        dkey_acc = dkey_acc + lax.dot_general(
            dscore_b, query, (((0,), (0,)), ((), ())), preferred_element_type=jnp.float32
        )
        dvalue_acc = dvalue_acc + lax.dot_general(
            probs_b, grad, (((0,), (0,)), ((), ())), preferred_element_type=jnp.float32
        )
    dkey_ref[...] = jnp.zeros(dkey_ref.shape, dkey_ref.dtype)
    dvalue_ref[...] = jnp.zeros(dvalue_ref.shape, dvalue_ref.dtype)
    dkey_ref[pl.ds(start, window), :] = dkey_acc * scale
    dvalue_ref[pl.ds(start, window), :] = dvalue_acc


def attention_forward(start, mask, query, keys, values, inputs, group_size):
    rows, width = query.shape
    seq_len, kv_width = keys.shape
    window = mask.shape[1]
    groups = kv_width // HD
    cols = group_size * HD
    kernel = functools.partial(forward_kernel, heads=group_size, scale=HD ** (-0.5))
    return pl.pallas_call(
        kernel,
        grid=(groups,),
        in_specs=[
            pl.BlockSpec(memory_space=pltpu.SMEM),
            pl.BlockSpec((rows, window), lambda g: (0, 0)),
            pl.BlockSpec((rows, cols), lambda g: (0, g)),
            pl.BlockSpec((seq_len, HD), lambda g: (0, g)),
            pl.BlockSpec((seq_len, HD), lambda g: (0, g)),
            pl.BlockSpec((rows, cols), lambda g: (0, g)),
        ],
        out_specs=pl.BlockSpec((rows, cols), lambda g: (0, g)),
        out_shape=jax.ShapeDtypeStruct((rows, width), jnp.bfloat16),
        interpret=INTERPRET,
    )(start, mask, query, keys, values, inputs)


def attention_backward(start, mask, query, keys, values, grad, group_size):
    rows, width = query.shape
    seq_len, kv_width = keys.shape
    window = mask.shape[1]
    groups = kv_width // HD
    cols = group_size * HD
    kernel = functools.partial(backward_kernel, heads=group_size, scale=HD ** (-0.5))
    return pl.pallas_call(
        kernel,
        grid=(groups,),
        in_specs=[
            pl.BlockSpec(memory_space=pltpu.SMEM),
            pl.BlockSpec((rows, window), lambda g: (0, 0)),
            pl.BlockSpec((rows, cols), lambda g: (0, g)),
            pl.BlockSpec((seq_len, HD), lambda g: (0, g)),
            pl.BlockSpec((seq_len, HD), lambda g: (0, g)),
            pl.BlockSpec((rows, cols), lambda g: (0, g)),
        ],
        out_specs=[
            pl.BlockSpec((rows, cols), lambda g: (0, g)),
            pl.BlockSpec((seq_len, HD), lambda g: (0, g)),
            pl.BlockSpec((seq_len, HD), lambda g: (0, g)),
        ],
        out_shape=[
            jax.ShapeDtypeStruct((rows, width), jnp.float32),
            jax.ShapeDtypeStruct((seq_len, kv_width), jnp.float32),
            jax.ShapeDtypeStruct((seq_len, kv_width), jnp.float32),
        ],
        interpret=INTERPRET,
    )(start, mask, query, keys, values, grad)


def body(sent_fwd, sent_grad, saved_bwd, norm_gain, key_proj, value_proj, seg_fwd, seg_bwd):
    tok_rows = sent_fwd.shape[1]
    width = sent_fwd.shape[2]
    kv_width = key_proj.shape[2]
    heads = width // HD
    kv_heads = kv_width // HD
    group_size = heads // kv_heads
    scale_factor = HD ** (-0.5)
    count = lax.axis_size("ctx")
    rank = lax.axis_index("ctx")
    offset = rank * tok_rows
    query_pos = offset + jnp.arange(tok_rows, dtype=jnp.int32)
    gain = norm_gain[0]
    key_weight = key_proj[0]
    value_weight = value_proj[0]
    arrived = shifted(sent_fwd, "section", 1)[0]
    upstream = shifted(sent_grad, "section", -1)[0]

    def layer_parts(inputs):
        normed, wide, inverse = normalize(inputs, gain)
        flat = normed.astype(jnp.bfloat16)
        keys = jnp.dot(flat, key_weight, preferred_element_type=jnp.float32).astype(jnp.bfloat16)
        values = jnp.dot(flat, value_weight, preferred_element_type=jnp.float32).astype(
            jnp.bfloat16
        )
        return (flat.reshape(tok_rows, heads, HD), keys, values, wide, inverse)

    def allowed_of(segment):
        seg_query = lax.dynamic_slice_in_dim(segment, offset, tok_rows)
        key_pos = jnp.arange(segment.shape[0], dtype=jnp.int32)
        return (key_pos[None, :] <= query_pos[:, None]) & (seg_query[:, None] == segment[None, :])

    back_blocks = -(-(SEGMENT_MAX - 1) // tok_rows)
    window = min(back_blocks + 1, count) * tok_rows
    window_start = jnp.minimum(jnp.maximum(rank - back_blocks, 0) * tok_rows, count * tok_rows - window)

    bwd_query, bwd_keys, bwd_values, bwd_wide, bwd_inverse = layer_parts(saved_bwd[0])
    bwd_all = gather_all(jnp.concatenate([bwd_keys, bwd_values], axis=1), "ctx")
    fwd_query, fwd_keys, fwd_values, fwd_wide, fwd_inverse = layer_parts(arrived)
    fwd_all = gather_all(jnp.concatenate([fwd_keys, fwd_values], axis=1), "ctx")

    bwd_key_all = bwd_all[:, :kv_width]
    bwd_value_all = bwd_all[:, kv_width:]
    allowed = lax.dynamic_slice_in_dim(allowed_of(seg_bwd).astype(jnp.int32), window_start, window, axis=1)
    start_row = window_start.reshape(1).astype(jnp.int32)
    halves = 2
    half_kv = kv_width // halves
    half_q = width // halves
    dquery_parts, dkey_parts, dvalue_parts = ([], [], [])
    half_terms = []
    for half in range(halves):
        kv_cols = slice(half * half_kv, (half + 1) * half_kv)
        q_cols = slice(half * half_q, (half + 1) * half_q)
        dquery_half, dkey_half, dvalue_half = attention_backward(
            start_row,
            allowed,
            bwd_query.reshape(tok_rows, width)[:, q_cols],
            bwd_key_all[:, kv_cols],
            bwd_value_all[:, kv_cols],
            upstream[:, q_cols],
            group_size,
        )
        dquery_parts.append(dquery_half)
        half_terms.append(jnp.concatenate([dkey_half, dvalue_half], axis=1))
    fwd_all, half_terms = lax.optimization_barrier((fwd_all, half_terms))
    for terms in half_terms:
        dkv_half = reduce_all(terms, "ctx").astype(jnp.bfloat16)
        dkey_parts.append(dkv_half[:, :half_kv])
        dvalue_parts.append(dkv_half[:, half_kv:])
    dquery = jnp.concatenate(dquery_parts, axis=1)
    dkeys = jnp.concatenate(dkey_parts, axis=1)
    dvalues = jnp.concatenate(dvalue_parts, axis=1)

    key_piece = fwd_all[:, :kv_width]
    value_piece = fwd_all[:, kv_width:]
    allowed = lax.dynamic_slice_in_dim(allowed_of(seg_fwd).astype(jnp.int32), window_start, window, axis=1)
    fwd_parts = []
    for half in range(halves):
        kv_cols = slice(half * half_kv, (half + 1) * half_kv)
        q_cols = slice(half * half_q, (half + 1) * half_q)
        fwd_parts.append(
            attention_forward(
                start_row,
                allowed,
                fwd_query.reshape(tok_rows, width)[:, q_cols],
                key_piece[:, kv_cols],
                value_piece[:, kv_cols],
                arrived[:, q_cols],
                group_size,
            )
        )
    fwd_out = jnp.concatenate(fwd_parts, axis=1)

    dnormed = dquery + jnp.dot(
        dkeys, jnp.transpose(key_weight), preferred_element_type=jnp.float32
    )
    dnormed = dnormed + jnp.dot(
        dvalues,
        jnp.transpose(value_weight),
        preferred_element_type=jnp.float32,
    )
    scaled = gain * dnormed
    grad_in = bwd_inverse * scaled - bwd_wide * bwd_inverse**3 * jnp.mean(
        bwd_wide * scaled, axis=-1, keepdims=True
    )
    grad_out = (upstream.astype(jnp.float32) + grad_in).astype(jnp.bfloat16)
    return (fwd_out[None], grad_out[None])


def solution(mesh):
    placed = (
        P("section", "ctx", None),
        P("section", "ctx", None),
        P("section", "ctx", None),
        P("section", None),
        P("section", None, None),
        P("section", None, None),
        P(),
        P(),
    )
    return jax.shard_map(
        body,
        mesh=mesh,
        in_specs=placed,
        out_specs=(P("section", "ctx", None), P("section", "ctx", None)),
        check_vma=False,
    )
```

```python
import functools

import jax
import jax.numpy as jnp
from jax import lax
from jax.sharding import PartitionSpec as P
from jax.experimental import pallas as pl
from jax.experimental.pallas import tpu as pltpu

HD = 128


EPSILON = 1e-05
NEGATIVE = -1e30
SEGMENT_MAX = 512


def shifted(block, axis, distance):
    devices = range(lax.axis_size(axis))
    route = [((i - distance) % len(devices), i) for i in devices]
    return lax.ppermute(block, axis, route)


def gather_all(block, axis):
    count = lax.axis_size(axis)
    spread = jnp.broadcast_to(block[None], (count,) + block.shape)
    moved = lax.all_to_all(spread, axis, 0, 0)
    return moved.reshape((count * block.shape[0],) + block.shape[1:])


def reduce_all(terms, axis):
    count = lax.axis_size(axis)
    rows = terms.shape[0] // count
    moved = lax.all_to_all(terms.astype(jnp.bfloat16).reshape((count, rows) + terms.shape[1:]), axis, 0, 0)
    return jnp.sum(moved.astype(jnp.float32), axis=0)


def normalize(inputs, gain):
    wide = inputs.astype(jnp.float32)
    inverse = lax.rsqrt(jnp.mean(wide * wide, axis=-1, keepdims=True) + EPSILON)
    return (wide * inverse * gain, wide, inverse)


INTERPRET = False


def forward_kernel(start_ref, mask_ref, query_ref, key_ref, value_ref, input_ref, out_ref, *, heads, scale):
    allowed = mask_ref[...] != 0
    window = mask_ref.shape[1]
    start = pl.multiple_of(start_ref[0], HD)
    keys = key_ref[pl.ds(start, window), :]
    values = value_ref[pl.ds(start, window), :]
    for head in range(heads):
        cols = slice(head * HD, (head + 1) * HD)
        scores = lax.dot_general(
            query_ref[:, cols], keys, (((1,), (1,)), ((), ())), preferred_element_type=jnp.float32
        ) * scale
        scores = jnp.where(allowed, scores, NEGATIVE)
        rowmax = jnp.max(scores, axis=1, keepdims=True)
        expo = jnp.where(allowed, jnp.exp(scores - rowmax), 0.0)
        total = jnp.sum(expo, axis=1, keepdims=True)
        product = jnp.dot(expo.astype(jnp.bfloat16), values, preferred_element_type=jnp.float32)
        out_ref[:, cols] = (input_ref[:, cols].astype(jnp.float32) + product / total).astype(out_ref.dtype)


def backward_kernel(start_ref, mask_ref, query_ref, key_ref, value_ref, grad_ref, dquery_ref, dkey_ref, dvalue_ref, *, heads, scale):
    allowed = mask_ref[...] != 0
    window = mask_ref.shape[1]
    start = pl.multiple_of(start_ref[0], HD)
    keys = key_ref[pl.ds(start, window), :]
    values = value_ref[pl.ds(start, window), :]
    dkey_acc = jnp.zeros((window, HD), jnp.float32)
    dvalue_acc = jnp.zeros((window, HD), jnp.float32)
    for head in range(heads):
        cols = slice(head * HD, (head + 1) * HD)
        query = query_ref[:, cols]
        grad = grad_ref[:, cols]
        scores = lax.dot_general(
            query, keys, (((1,), (1,)), ((), ())), preferred_element_type=jnp.float32
        ) * scale
        scores = jnp.where(allowed, scores, NEGATIVE)
        rowmax = jnp.max(scores, axis=1, keepdims=True)
        expo = jnp.where(allowed, jnp.exp(scores - rowmax), 0.0)
        total = jnp.sum(expo, axis=1, keepdims=True)
        probs = expo / total
        dprob = lax.dot_general(
            grad, values, (((1,), (1,)), ((), ())), preferred_element_type=jnp.float32
        )
        delta = jnp.sum(probs * dprob, axis=1, keepdims=True)
        dscore_b = (probs * (dprob - delta)).astype(jnp.bfloat16)
        probs_b = probs.astype(jnp.bfloat16)
        dquery_ref[:, cols] = jnp.dot(dscore_b, keys, preferred_element_type=jnp.float32) * scale
        dkey_acc = dkey_acc + lax.dot_general(
            dscore_b, query, (((0,), (0,)), ((), ())), preferred_element_type=jnp.float32
        )
        dvalue_acc = dvalue_acc + lax.dot_general(
            probs_b, grad, (((0,), (0,)), ((), ())), preferred_element_type=jnp.float32
        )
    dkey_ref[...] = jnp.zeros(dkey_ref.shape, dkey_ref.dtype)
    dvalue_ref[...] = jnp.zeros(dvalue_ref.shape, dvalue_ref.dtype)
    dkey_ref[pl.ds(start, window), :] = dkey_acc * scale
    dvalue_ref[pl.ds(start, window), :] = dvalue_acc


def attention_forward(start, mask, query, keys, values, inputs, group_size):
    rows, width = query.shape
    seq_len, kv_width = keys.shape
    window = mask.shape[1]
    groups = kv_width // HD
    cols = group_size * HD
    kernel = functools.partial(forward_kernel, heads=group_size, scale=HD ** (-0.5))
    return pl.pallas_call(
        kernel,
        grid=(groups,),
        in_specs=[
            pl.BlockSpec(memory_space=pltpu.SMEM),
            pl.BlockSpec((rows, window), lambda g: (0, 0)),
            pl.BlockSpec((rows, cols), lambda g: (0, g)),
            pl.BlockSpec((seq_len, HD), lambda g: (0, g)),
            pl.BlockSpec((seq_len, HD), lambda g: (0, g)),
            pl.BlockSpec((rows, cols), lambda g: (0, g)),
        ],
        out_specs=pl.BlockSpec((rows, cols), lambda g: (0, g)),
        out_shape=jax.ShapeDtypeStruct((rows, width), jnp.bfloat16),
        interpret=INTERPRET,
    )(start, mask, query, keys, values, inputs)


def attention_backward(start, mask, query, keys, values, grad, group_size):
    rows, width = query.shape
    seq_len, kv_width = keys.shape
    window = mask.shape[1]
    groups = kv_width // HD
    cols = group_size * HD
    kernel = functools.partial(backward_kernel, heads=group_size, scale=HD ** (-0.5))
    return pl.pallas_call(
        kernel,
        grid=(groups,),
        in_specs=[
            pl.BlockSpec(memory_space=pltpu.SMEM),
            pl.BlockSpec((rows, window), lambda g: (0, 0)),
            pl.BlockSpec((rows, cols), lambda g: (0, g)),
            pl.BlockSpec((seq_len, HD), lambda g: (0, g)),
            pl.BlockSpec((seq_len, HD), lambda g: (0, g)),
            pl.BlockSpec((rows, cols), lambda g: (0, g)),
        ],
        out_specs=[
            pl.BlockSpec((rows, cols), lambda g: (0, g)),
            pl.BlockSpec((seq_len, HD), lambda g: (0, g)),
            pl.BlockSpec((seq_len, HD), lambda g: (0, g)),
        ],
        out_shape=[
            jax.ShapeDtypeStruct((rows, width), jnp.float32),
            jax.ShapeDtypeStruct((seq_len, kv_width), jnp.float32),
            jax.ShapeDtypeStruct((seq_len, kv_width), jnp.float32),
        ],
        interpret=INTERPRET,
    )(start, mask, query, keys, values, grad)


def body(sent_fwd, sent_grad, saved_bwd, norm_gain, key_proj, value_proj, seg_fwd, seg_bwd):
    tok_rows = sent_fwd.shape[1]
    width = sent_fwd.shape[2]
    kv_width = key_proj.shape[2]
    heads = width // HD
    kv_heads = kv_width // HD
    group_size = heads // kv_heads
    scale_factor = HD ** (-0.5)
    count = lax.axis_size("ctx")
    rank = lax.axis_index("ctx")
    offset = rank * tok_rows
    query_pos = offset + jnp.arange(tok_rows, dtype=jnp.int32)
    gain = norm_gain[0]
    key_weight = key_proj[0]
    value_weight = value_proj[0]
    arrived = shifted(sent_fwd, "section", 1)[0]
    upstream = shifted(sent_grad, "section", -1)[0]

    def layer_parts(inputs):
        normed, wide, inverse = normalize(inputs, gain)
        flat = normed.astype(jnp.bfloat16)
        keys = jnp.dot(flat, key_weight, preferred_element_type=jnp.float32).astype(jnp.bfloat16)
        values = jnp.dot(flat, value_weight, preferred_element_type=jnp.float32).astype(
            jnp.bfloat16
        )
        return (flat.reshape(tok_rows, heads, HD), keys, values, wide, inverse)

    def allowed_of(segment):
        seg_query = lax.dynamic_slice_in_dim(segment, offset, tok_rows)
        key_pos = jnp.arange(segment.shape[0], dtype=jnp.int32)
        return (key_pos[None, :] <= query_pos[:, None]) & (seg_query[:, None] == segment[None, :])

    back_blocks = -(-(SEGMENT_MAX - 1) // tok_rows)
    window = min(back_blocks + 1, count) * tok_rows
    window_start = jnp.minimum(jnp.maximum(rank - back_blocks, 0) * tok_rows, count * tok_rows - window)

    bwd_query, bwd_keys, bwd_values, bwd_wide, bwd_inverse = layer_parts(saved_bwd[0])
    bwd_all = gather_all(jnp.concatenate([bwd_keys, bwd_values], axis=1), "ctx")
    fwd_query, fwd_keys, fwd_values, fwd_wide, fwd_inverse = layer_parts(arrived)
    fwd_all = gather_all(jnp.concatenate([fwd_keys, fwd_values], axis=1), "ctx")

    bwd_key_all = bwd_all[:, :kv_width]
    bwd_value_all = bwd_all[:, kv_width:]
    allowed = lax.dynamic_slice_in_dim(allowed_of(seg_bwd).astype(jnp.int32), window_start, window, axis=1)
    start_row = window_start.reshape(1).astype(jnp.int32)
    halves = 2
    half_kv = kv_width // halves
    half_q = width // halves
    dquery_parts, dkey_parts, dvalue_parts = ([], [], [])
    half_terms = []
    for half in range(halves):
        kv_cols = slice(half * half_kv, (half + 1) * half_kv)
        q_cols = slice(half * half_q, (half + 1) * half_q)
        dquery_half, dkey_half, dvalue_half = attention_backward(
            start_row,
            allowed,
            bwd_query.reshape(tok_rows, width)[:, q_cols],
            bwd_key_all[:, kv_cols],
            bwd_value_all[:, kv_cols],
            upstream[:, q_cols],
            group_size,
        )
        dquery_parts.append(dquery_half)
        half_terms.append(jnp.concatenate([dkey_half, dvalue_half], axis=1))
    fwd_all, half_terms = lax.optimization_barrier((fwd_all, half_terms))

    key_piece = fwd_all[:, :kv_width]
    value_piece = fwd_all[:, kv_width:]
    allowed = lax.dynamic_slice_in_dim(allowed_of(seg_fwd).astype(jnp.int32), window_start, window, axis=1)
    dkv_all = reduce_all(jnp.concatenate(half_terms, axis=1), "ctx").astype(jnp.bfloat16)
    for half in range(halves):
        base = half * 2 * half_kv
        dkey_parts.append(dkv_all[:, base:base + half_kv])
        dvalue_parts.append(dkv_all[:, base + half_kv:base + 2 * half_kv])
    dquery = jnp.concatenate(dquery_parts, axis=1)
    dkeys = jnp.concatenate(dkey_parts, axis=1)
    dvalues = jnp.concatenate(dvalue_parts, axis=1)
    fwd_parts = []
    for half in range(halves):
        kv_cols = slice(half * half_kv, (half + 1) * half_kv)
        q_cols = slice(half * half_q, (half + 1) * half_q)
        fwd_parts.append(
            attention_forward(
                start_row,
                allowed,
                fwd_query.reshape(tok_rows, width)[:, q_cols],
                key_piece[:, kv_cols],
                value_piece[:, kv_cols],
                arrived[:, q_cols],
                group_size,
            )
        )
    fwd_out = jnp.concatenate(fwd_parts, axis=1)

    dnormed = dquery + jnp.dot(
        dkeys, jnp.transpose(key_weight), preferred_element_type=jnp.float32
    )
    dnormed = dnormed + jnp.dot(
        dvalues,
        jnp.transpose(value_weight),
        preferred_element_type=jnp.float32,
    )
    scaled = gain * dnormed
    grad_in = bwd_inverse * scaled - bwd_wide * bwd_inverse**3 * jnp.mean(
        bwd_wide * scaled, axis=-1, keepdims=True
    )
    grad_out = (upstream.astype(jnp.float32) + grad_in).astype(jnp.bfloat16)
    return (fwd_out[None], grad_out[None])


def solution(mesh):
    placed = (
        P("section", "ctx", None),
        P("section", "ctx", None),
        P("section", "ctx", None),
        P("section", None),
        P("section", None, None),
        P("section", None, None),
        P(),
        P(),
    )
    return jax.shard_map(
        body,
        mesh=mesh,
        in_specs=placed,
        out_specs=(P("section", "ctx", None), P("section", "ctx", None)),
        check_vma=False,
    )
```

```python
import functools

import jax
import jax.numpy as jnp
from jax import lax
from jax.sharding import PartitionSpec as P
from jax.experimental import pallas as pl
from jax.experimental.pallas import tpu as pltpu

HD = 128


EPSILON = 1e-05
NEGATIVE = -1e30
SEGMENT_MAX = 512


def shifted(block, axis, distance):
    devices = range(lax.axis_size(axis))
    route = [((i - distance) % len(devices), i) for i in devices]
    return lax.ppermute(block, axis, route)


def gather_all(block, axis):
    count = lax.axis_size(axis)
    spread = jnp.broadcast_to(block[None], (count,) + block.shape)
    moved = lax.all_to_all(spread, axis, 0, 0)
    return moved.reshape((count * block.shape[0],) + block.shape[1:])


def reduce_all(terms, axis):
    count = lax.axis_size(axis)
    rows = terms.shape[0] // count
    moved = lax.all_to_all(terms.astype(jnp.bfloat16).reshape((count, rows) + terms.shape[1:]), axis, 0, 0)
    return jnp.sum(moved.astype(jnp.float32), axis=0)


def normalize(inputs, gain):
    wide = inputs.astype(jnp.float32)
    inverse = lax.rsqrt(jnp.mean(wide * wide, axis=-1, keepdims=True) + EPSILON)
    return (wide * inverse * gain, wide, inverse)


INTERPRET = False


def forward_kernel(start_ref, mask_ref, query_ref, key_ref, value_ref, input_ref, out_ref, *, heads, scale):
    allowed = mask_ref[...] != 0
    window = mask_ref.shape[1]
    start = pl.multiple_of(start_ref[0], HD)
    keys = key_ref[pl.ds(start, window), :]
    values = value_ref[pl.ds(start, window), :]
    for head in range(heads):
        cols = slice(head * HD, (head + 1) * HD)
        scores = lax.dot_general(
            query_ref[:, cols], keys, (((1,), (1,)), ((), ())), preferred_element_type=jnp.float32
        ) * scale
        scores = jnp.where(allowed, scores, NEGATIVE)
        rowmax = jnp.max(scores, axis=1, keepdims=True)
        expo = jnp.exp(scores - rowmax)
        total = jnp.sum(expo, axis=1, keepdims=True)
        product = jnp.dot(expo.astype(jnp.bfloat16), values, preferred_element_type=jnp.float32)
        out_ref[:, cols] = (input_ref[:, cols].astype(jnp.float32) + product / total).astype(out_ref.dtype)


def backward_kernel(start_ref, mask_ref, query_ref, key_ref, value_ref, grad_ref, dquery_ref, dkey_ref, dvalue_ref, *, heads, scale):
    allowed = mask_ref[...] != 0
    window = mask_ref.shape[1]
    start = pl.multiple_of(start_ref[0], HD)
    keys = key_ref[pl.ds(start, window), :]
    values = value_ref[pl.ds(start, window), :]
    dkey_acc = jnp.zeros((window, HD), jnp.float32)
    dvalue_acc = jnp.zeros((window, HD), jnp.float32)
    for head in range(heads):
        cols = slice(head * HD, (head + 1) * HD)
        query = query_ref[:, cols]
        grad = grad_ref[:, cols]
        scores = lax.dot_general(
            query, keys, (((1,), (1,)), ((), ())), preferred_element_type=jnp.float32
        ) * scale
        scores = jnp.where(allowed, scores, NEGATIVE)
        rowmax = jnp.max(scores, axis=1, keepdims=True)
        expo = jnp.exp(scores - rowmax)
        total = jnp.sum(expo, axis=1, keepdims=True)
        probs = expo * (1.0 / total)
        dprob = lax.dot_general(
            grad, values, (((1,), (1,)), ((), ())), preferred_element_type=jnp.float32
        )
        delta = jnp.sum(probs * dprob, axis=1, keepdims=True)
        dscore_b = (probs * (dprob - delta)).astype(jnp.bfloat16)
        probs_b = probs.astype(jnp.bfloat16)
        dquery_ref[:, cols] = jnp.dot(dscore_b, keys, preferred_element_type=jnp.float32) * scale
        dkey_acc = dkey_acc + lax.dot_general(
            dscore_b, query, (((0,), (0,)), ((), ())), preferred_element_type=jnp.float32
        )
        dvalue_acc = dvalue_acc + lax.dot_general(
            probs_b, grad, (((0,), (0,)), ((), ())), preferred_element_type=jnp.float32
        )
    dkey_ref[...] = jnp.zeros(dkey_ref.shape, dkey_ref.dtype)
    dvalue_ref[...] = jnp.zeros(dvalue_ref.shape, dvalue_ref.dtype)
    dkey_ref[pl.ds(start, window), :] = dkey_acc * scale
    dvalue_ref[pl.ds(start, window), :] = dvalue_acc


def attention_forward(start, mask, query, keys, values, inputs, group_size):
    rows, width = query.shape
    seq_len, kv_width = keys.shape
    window = mask.shape[1]
    groups = kv_width // HD
    cols = group_size * HD
    kernel = functools.partial(forward_kernel, heads=group_size, scale=HD ** (-0.5))
    return pl.pallas_call(
        kernel,
        grid=(groups,),
        in_specs=[
            pl.BlockSpec(memory_space=pltpu.SMEM),
            pl.BlockSpec((rows, window), lambda g: (0, 0)),
            pl.BlockSpec((rows, cols), lambda g: (0, g)),
            pl.BlockSpec((seq_len, HD), lambda g: (0, g)),
            pl.BlockSpec((seq_len, HD), lambda g: (0, g)),
            pl.BlockSpec((rows, cols), lambda g: (0, g)),
        ],
        out_specs=pl.BlockSpec((rows, cols), lambda g: (0, g)),
        out_shape=jax.ShapeDtypeStruct((rows, width), jnp.bfloat16),
        interpret=INTERPRET,
    )(start, mask, query, keys, values, inputs)


def attention_backward(start, mask, query, keys, values, grad, group_size):
    rows, width = query.shape
    seq_len, kv_width = keys.shape
    window = mask.shape[1]
    groups = kv_width // HD
    cols = group_size * HD
    kernel = functools.partial(backward_kernel, heads=group_size, scale=HD ** (-0.5))
    return pl.pallas_call(
        kernel,
        grid=(groups,),
        in_specs=[
            pl.BlockSpec(memory_space=pltpu.SMEM),
            pl.BlockSpec((rows, window), lambda g: (0, 0)),
            pl.BlockSpec((rows, cols), lambda g: (0, g)),
            pl.BlockSpec((seq_len, HD), lambda g: (0, g)),
            pl.BlockSpec((seq_len, HD), lambda g: (0, g)),
            pl.BlockSpec((rows, cols), lambda g: (0, g)),
        ],
        out_specs=[
            pl.BlockSpec((rows, cols), lambda g: (0, g)),
            pl.BlockSpec((seq_len, HD), lambda g: (0, g)),
            pl.BlockSpec((seq_len, HD), lambda g: (0, g)),
        ],
        out_shape=[
            jax.ShapeDtypeStruct((rows, width), jnp.float32),
            jax.ShapeDtypeStruct((seq_len, kv_width), jnp.float32),
            jax.ShapeDtypeStruct((seq_len, kv_width), jnp.float32),
        ],
        interpret=INTERPRET,
    )(start, mask, query, keys, values, grad)


def body(sent_fwd, sent_grad, saved_bwd, norm_gain, key_proj, value_proj, seg_fwd, seg_bwd):
    tok_rows = sent_fwd.shape[1]
    width = sent_fwd.shape[2]
    kv_width = key_proj.shape[2]
    heads = width // HD
    kv_heads = kv_width // HD
    group_size = heads // kv_heads
    scale_factor = HD ** (-0.5)
    count = lax.axis_size("ctx")
    rank = lax.axis_index("ctx")
    offset = rank * tok_rows
    query_pos = offset + jnp.arange(tok_rows, dtype=jnp.int32)
    gain = norm_gain[0]
    key_weight = key_proj[0]
    value_weight = value_proj[0]
    arrived = shifted(sent_fwd, "section", 1)[0]
    upstream = shifted(sent_grad, "section", -1)[0]

    def layer_parts(inputs):
        normed, wide, inverse = normalize(inputs, gain)
        flat = normed.astype(jnp.bfloat16)
        keys = jnp.dot(flat, key_weight, preferred_element_type=jnp.float32).astype(jnp.bfloat16)
        values = jnp.dot(flat, value_weight, preferred_element_type=jnp.float32).astype(
            jnp.bfloat16
        )
        return (flat.reshape(tok_rows, heads, HD), keys, values, wide, inverse)

    def allowed_of(segment):
        seg_query = lax.dynamic_slice_in_dim(segment, offset, tok_rows)
        key_pos = jnp.arange(segment.shape[0], dtype=jnp.int32)
        return (key_pos[None, :] <= query_pos[:, None]) & (seg_query[:, None] == segment[None, :])

    back_blocks = -(-(SEGMENT_MAX - 1) // tok_rows)
    window = min(back_blocks + 1, count) * tok_rows
    window_start = jnp.minimum(jnp.maximum(rank - back_blocks, 0) * tok_rows, count * tok_rows - window)

    bwd_query, bwd_keys, bwd_values, bwd_wide, bwd_inverse = layer_parts(saved_bwd[0])
    bwd_all = gather_all(jnp.concatenate([bwd_keys, bwd_values], axis=1), "ctx")
    fwd_query, fwd_keys, fwd_values, fwd_wide, fwd_inverse = layer_parts(arrived)
    fwd_all = gather_all(jnp.concatenate([fwd_keys, fwd_values], axis=1), "ctx")

    bwd_key_all = bwd_all[:, :kv_width]
    bwd_value_all = bwd_all[:, kv_width:]
    allowed = lax.dynamic_slice_in_dim(allowed_of(seg_bwd).astype(jnp.int32), window_start, window, axis=1)
    start_row = window_start.reshape(1).astype(jnp.int32)
    halves = 2
    half_kv = kv_width // halves
    half_q = width // halves
    dquery_parts, dkey_parts, dvalue_parts = ([], [], [])
    half_terms = []
    for half in range(halves):
        kv_cols = slice(half * half_kv, (half + 1) * half_kv)
        q_cols = slice(half * half_q, (half + 1) * half_q)
        dquery_half, dkey_half, dvalue_half = attention_backward(
            start_row,
            allowed,
            bwd_query.reshape(tok_rows, width)[:, q_cols],
            bwd_key_all[:, kv_cols],
            bwd_value_all[:, kv_cols],
            upstream[:, q_cols],
            group_size,
        )
        dquery_parts.append(dquery_half)
        half_terms.append(jnp.concatenate([dkey_half, dvalue_half], axis=1))
    fwd_all, half_terms = lax.optimization_barrier((fwd_all, half_terms))

    key_piece = fwd_all[:, :kv_width]
    value_piece = fwd_all[:, kv_width:]
    allowed = lax.dynamic_slice_in_dim(allowed_of(seg_fwd).astype(jnp.int32), window_start, window, axis=1)
    dkv_all = reduce_all(jnp.concatenate(half_terms, axis=1), "ctx").astype(jnp.bfloat16)
    for half in range(halves):
        base = half * 2 * half_kv
        dkey_parts.append(dkv_all[:, base:base + half_kv])
        dvalue_parts.append(dkv_all[:, base + half_kv:base + 2 * half_kv])
    dquery = jnp.concatenate(dquery_parts, axis=1)
    dkeys = jnp.concatenate(dkey_parts, axis=1)
    dvalues = jnp.concatenate(dvalue_parts, axis=1)
    fwd_parts = []
    for half in range(halves):
        kv_cols = slice(half * half_kv, (half + 1) * half_kv)
        q_cols = slice(half * half_q, (half + 1) * half_q)
        fwd_parts.append(
            attention_forward(
                start_row,
                allowed,
                fwd_query.reshape(tok_rows, width)[:, q_cols],
                key_piece[:, kv_cols],
                value_piece[:, kv_cols],
                arrived[:, q_cols],
                group_size,
            )
        )
    fwd_out = jnp.concatenate(fwd_parts, axis=1)

    dnormed = dquery + jnp.dot(
        dkeys, jnp.transpose(key_weight), preferred_element_type=jnp.float32
    )
    dnormed = dnormed + jnp.dot(
        dvalues,
        jnp.transpose(value_weight),
        preferred_element_type=jnp.float32,
    )
    scaled = gain * dnormed
    grad_in = bwd_inverse * scaled - bwd_wide * bwd_inverse**3 * jnp.mean(
        bwd_wide * scaled, axis=-1, keepdims=True
    )
    grad_out = (upstream.astype(jnp.float32) + grad_in).astype(jnp.bfloat16)
    return (fwd_out[None], grad_out[None])


def solution(mesh):
    placed = (
        P("section", "ctx", None),
        P("section", "ctx", None),
        P("section", "ctx", None),
        P("section", None),
        P("section", None, None),
        P("section", None, None),
        P(),
        P(),
    )
    return jax.shard_map(
        body,
        mesh=mesh,
        in_specs=placed,
        out_specs=(P("section", "ctx", None), P("section", "ctx", None)),
        check_vma=False,
    )
```

```python
import functools

import jax
import jax.numpy as jnp
from jax import lax
from jax.sharding import PartitionSpec as P
from jax.experimental import pallas as pl
from jax.experimental.pallas import tpu as pltpu

HD = 128


EPSILON = 1e-05
NEGATIVE = -1e30
SEGMENT_MAX = 512


def shifted(block, axis, distance):
    devices = range(lax.axis_size(axis))
    route = [((i - distance) % len(devices), i) for i in devices]
    return lax.ppermute(block, axis, route)


def gather_all(block, axis):
    count = lax.axis_size(axis)
    spread = jnp.broadcast_to(block[None], (count,) + block.shape)
    moved = lax.all_to_all(spread, axis, 0, 0)
    return moved.reshape((count * block.shape[0],) + block.shape[1:])


def reduce_all(terms, axis):
    count = lax.axis_size(axis)
    rows = terms.shape[0] // count
    moved = lax.all_to_all(terms.astype(jnp.bfloat16).reshape((count, rows) + terms.shape[1:]), axis, 0, 0)
    return jnp.sum(moved.astype(jnp.float32), axis=0)


def normalize(inputs, gain):
    wide = inputs.astype(jnp.float32)
    inverse = lax.rsqrt(jnp.mean(wide * wide, axis=-1, keepdims=True) + EPSILON)
    return (wide * inverse * gain, wide, inverse)


INTERPRET = False


def forward_kernel(start_ref, mask_ref, query_ref, key_ref, value_ref, input_ref, out_ref, *, heads, scale):
    allowed = mask_ref[...] != 0
    window = mask_ref.shape[1]
    start = pl.multiple_of(start_ref[0], HD)
    keys = key_ref[pl.ds(start, window), :]
    values = value_ref[pl.ds(start, window), :]
    for head in range(heads):
        cols = slice(head * HD, (head + 1) * HD)
        scores = lax.dot_general(
            query_ref[:, cols], keys, (((1,), (1,)), ((), ())), preferred_element_type=jnp.float32
        ) * scale
        scores = jnp.where(allowed, scores, NEGATIVE)
        rowmax = jnp.max(scores, axis=1, keepdims=True)
        expo = jnp.where(allowed, jnp.exp(scores - rowmax), 0.0)
        total = jnp.sum(expo, axis=1, keepdims=True)
        product = jnp.dot(expo.astype(jnp.bfloat16), values, preferred_element_type=jnp.float32)
        out_ref[:, cols] = (input_ref[:, cols].astype(jnp.float32) + product / total).astype(out_ref.dtype)


def backward_kernel(start_ref, mask_ref, query_ref, key_ref, value_ref, grad_ref, dquery_ref, dkey_ref, dvalue_ref, *, heads, scale):
    allowed = mask_ref[...] != 0
    window = mask_ref.shape[1]
    start = pl.multiple_of(start_ref[0], HD)
    keys = key_ref[pl.ds(start, window), :]
    values = value_ref[pl.ds(start, window), :]
    dkey_acc = jnp.zeros((window, HD), jnp.float32)
    dvalue_acc = jnp.zeros((window, HD), jnp.float32)
    for head in range(heads):
        cols = slice(head * HD, (head + 1) * HD)
        query = query_ref[:, cols]
        grad = grad_ref[:, cols]
        scores = lax.dot_general(
            query, keys, (((1,), (1,)), ((), ())), preferred_element_type=jnp.float32
        ) * scale
        scores = jnp.where(allowed, scores, NEGATIVE)
        rowmax = jnp.max(scores, axis=1, keepdims=True)
        expo = jnp.where(allowed, jnp.exp(scores - rowmax), 0.0)
        total = jnp.sum(expo, axis=1, keepdims=True)
        probs = expo / total
        dprob = lax.dot_general(
            grad, values, (((1,), (1,)), ((), ())), preferred_element_type=jnp.float32
        )
        delta = jnp.sum(probs * dprob, axis=1, keepdims=True)
        dscore_b = (probs * (dprob - delta)).astype(jnp.bfloat16)
        probs_b = probs.astype(jnp.bfloat16)
        dquery_ref[:, cols] = jnp.dot(dscore_b, keys, preferred_element_type=jnp.float32) * scale
        dkey_acc = dkey_acc + lax.dot_general(
            dscore_b, query, (((0,), (0,)), ((), ())), preferred_element_type=jnp.float32
        )
        dvalue_acc = dvalue_acc + lax.dot_general(
            probs_b, grad, (((0,), (0,)), ((), ())), preferred_element_type=jnp.float32
        )
    dkey_ref[...] = jnp.zeros(dkey_ref.shape, dkey_ref.dtype)
    dvalue_ref[...] = jnp.zeros(dvalue_ref.shape, dvalue_ref.dtype)
    dkey_ref[pl.ds(start, window), :] = dkey_acc * scale
    dvalue_ref[pl.ds(start, window), :] = dvalue_acc


def attention_forward(start, mask, query, keys, values, inputs, group_size):
    rows, width = query.shape
    seq_len, kv_width = keys.shape
    window = mask.shape[1]
    groups = kv_width // HD
    cols = group_size * HD
    kernel = functools.partial(forward_kernel, heads=group_size, scale=HD ** (-0.5))
    return pl.pallas_call(
        kernel,
        grid=(groups,),
        in_specs=[
            pl.BlockSpec(memory_space=pltpu.SMEM),
            pl.BlockSpec((rows, window), lambda g: (0, 0)),
            pl.BlockSpec((rows, cols), lambda g: (0, g)),
            pl.BlockSpec((seq_len, HD), lambda g: (0, g)),
            pl.BlockSpec((seq_len, HD), lambda g: (0, g)),
            pl.BlockSpec((rows, cols), lambda g: (0, g)),
        ],
        out_specs=pl.BlockSpec((rows, cols), lambda g: (0, g)),
        out_shape=jax.ShapeDtypeStruct((rows, width), jnp.bfloat16),
        interpret=INTERPRET,
    )(start, mask, query, keys, values, inputs)


def attention_backward(start, mask, query, keys, values, grad, group_size):
    rows, width = query.shape
    seq_len, kv_width = keys.shape
    window = mask.shape[1]
    groups = kv_width // HD
    cols = group_size * HD
    kernel = functools.partial(backward_kernel, heads=group_size, scale=HD ** (-0.5))
    return pl.pallas_call(
        kernel,
        grid=(groups,),
        in_specs=[
            pl.BlockSpec(memory_space=pltpu.SMEM),
            pl.BlockSpec((rows, window), lambda g: (0, 0)),
            pl.BlockSpec((rows, cols), lambda g: (0, g)),
            pl.BlockSpec((seq_len, HD), lambda g: (0, g)),
            pl.BlockSpec((seq_len, HD), lambda g: (0, g)),
            pl.BlockSpec((rows, cols), lambda g: (0, g)),
        ],
        out_specs=[
            pl.BlockSpec((rows, cols), lambda g: (0, g)),
            pl.BlockSpec((seq_len, HD), lambda g: (0, g)),
            pl.BlockSpec((seq_len, HD), lambda g: (0, g)),
        ],
        out_shape=[
            jax.ShapeDtypeStruct((rows, width), jnp.float32),
            jax.ShapeDtypeStruct((seq_len, kv_width), jnp.float32),
            jax.ShapeDtypeStruct((seq_len, kv_width), jnp.float32),
        ],
        interpret=INTERPRET,
    )(start, mask, query, keys, values, grad)


def body(sent_fwd, sent_grad, saved_bwd, norm_gain, key_proj, value_proj, seg_fwd, seg_bwd):
    tok_rows = sent_fwd.shape[1]
    width = sent_fwd.shape[2]
    kv_width = key_proj.shape[2]
    heads = width // HD
    kv_heads = kv_width // HD
    group_size = heads // kv_heads
    scale_factor = HD ** (-0.5)
    count = lax.axis_size("ctx")
    rank = lax.axis_index("ctx")
    offset = rank * tok_rows
    query_pos = offset + jnp.arange(tok_rows, dtype=jnp.int32)
    gain = norm_gain[0]
    key_weight = key_proj[0]
    value_weight = value_proj[0]
    arrived = shifted(sent_fwd, "section", 1)[0]
    upstream = shifted(sent_grad, "section", -1)[0]

    def layer_parts(inputs):
        normed, wide, inverse = normalize(inputs, gain)
        flat = normed.astype(jnp.bfloat16)
        keys = jnp.dot(flat, key_weight, preferred_element_type=jnp.float32).astype(jnp.bfloat16)
        values = jnp.dot(flat, value_weight, preferred_element_type=jnp.float32).astype(
            jnp.bfloat16
        )
        return (flat.reshape(tok_rows, heads, HD), keys, values, wide, inverse)

    def allowed_of(segment):
        seg_query = lax.dynamic_slice_in_dim(segment, offset, tok_rows)
        key_pos = jnp.arange(segment.shape[0], dtype=jnp.int32)
        return (key_pos[None, :] <= query_pos[:, None]) & (seg_query[:, None] == segment[None, :])

    back_blocks = -(-(SEGMENT_MAX - 1) // tok_rows)
    window = min(back_blocks + 1, count) * tok_rows
    window_start = jnp.minimum(jnp.maximum(rank - back_blocks, 0) * tok_rows, count * tok_rows - window)

    bwd_query, bwd_keys, bwd_values, bwd_wide, bwd_inverse = layer_parts(saved_bwd[0])
    bwd_all = gather_all(jnp.concatenate([bwd_keys, bwd_values], axis=1), "ctx")
    fwd_query, fwd_keys, fwd_values, fwd_wide, fwd_inverse = layer_parts(arrived)
    fwd_all = gather_all(jnp.concatenate([fwd_keys, fwd_values], axis=1), "ctx")

    bwd_key_all = bwd_all[:, :kv_width]
    bwd_value_all = bwd_all[:, kv_width:]
    allowed = lax.dynamic_slice_in_dim(allowed_of(seg_bwd).astype(jnp.int32), window_start, window, axis=1)
    start_row = window_start.reshape(1).astype(jnp.int32)
    halves = 2
    fwd_halves = 1
    half_kv = kv_width // halves
    half_q = width // halves
    dquery_parts, dkey_parts, dvalue_parts = ([], [], [])
    half_terms = []
    for half in range(halves):
        kv_cols = slice(half * half_kv, (half + 1) * half_kv)
        q_cols = slice(half * half_q, (half + 1) * half_q)
        dquery_half, dkey_half, dvalue_half = attention_backward(
            start_row,
            allowed,
            bwd_query.reshape(tok_rows, width)[:, q_cols],
            bwd_key_all[:, kv_cols],
            bwd_value_all[:, kv_cols],
            upstream[:, q_cols],
            group_size,
        )
        dquery_parts.append(dquery_half)
        half_terms.append(jnp.concatenate([dkey_half, dvalue_half], axis=1))
    fwd_all, half_terms = lax.optimization_barrier((fwd_all, half_terms))

    key_piece = fwd_all[:, :kv_width]
    value_piece = fwd_all[:, kv_width:]
    allowed = lax.dynamic_slice_in_dim(allowed_of(seg_fwd).astype(jnp.int32), window_start, window, axis=1)
    dkv_all = reduce_all(jnp.concatenate(half_terms, axis=1), "ctx").astype(jnp.bfloat16)
    for half in range(halves):
        base = half * 2 * half_kv
        dkey_parts.append(dkv_all[:, base:base + half_kv])
        dvalue_parts.append(dkv_all[:, base + half_kv:base + 2 * half_kv])
    dquery = jnp.concatenate(dquery_parts, axis=1)
    dkeys = jnp.concatenate(dkey_parts, axis=1)
    dvalues = jnp.concatenate(dvalue_parts, axis=1)
    fwd_parts = []
    fwd_kv = kv_width // fwd_halves
    fwd_q = width // fwd_halves
    for half in range(fwd_halves):
        kv_cols = slice(half * fwd_kv, (half + 1) * fwd_kv)
        q_cols = slice(half * fwd_q, (half + 1) * fwd_q)
        fwd_parts.append(
            attention_forward(
                start_row,
                allowed,
                fwd_query.reshape(tok_rows, width)[:, q_cols],
                key_piece[:, kv_cols],
                value_piece[:, kv_cols],
                arrived[:, q_cols],
                group_size,
            )
        )
    fwd_out = jnp.concatenate(fwd_parts, axis=1)

    dnormed = dquery + jnp.dot(
        dkeys, jnp.transpose(key_weight), preferred_element_type=jnp.float32
    )
    dnormed = dnormed + jnp.dot(
        dvalues,
        jnp.transpose(value_weight),
        preferred_element_type=jnp.float32,
    )
    scaled = gain * dnormed
    grad_in = bwd_inverse * scaled - bwd_wide * bwd_inverse**3 * jnp.mean(
        bwd_wide * scaled, axis=-1, keepdims=True
    )
    grad_out = (upstream.astype(jnp.float32) + grad_in).astype(jnp.bfloat16)
    return (fwd_out[None], grad_out[None])


def solution(mesh):
    placed = (
        P("section", "ctx", None),
        P("section", "ctx", None),
        P("section", "ctx", None),
        P("section", None),
        P("section", None, None),
        P("section", None, None),
        P(),
        P(),
    )
    return jax.shard_map(
        body,
        mesh=mesh,
        in_specs=placed,
        out_specs=(P("section", "ctx", None), P("section", "ctx", None)),
        check_vma=False,
    )
```

```python
import functools

import jax
import jax.numpy as jnp
from jax import lax
from jax.sharding import PartitionSpec as P
from jax.experimental import pallas as pl
from jax.experimental.pallas import tpu as pltpu

HD = 128


EPSILON = 1e-05
NEGATIVE = -1e30
SEGMENT_MAX = 512


def shifted(block, axis, distance):
    devices = range(lax.axis_size(axis))
    route = [((i - distance) % len(devices), i) for i in devices]
    return lax.ppermute(block, axis, route)


def gather_all(block, axis):
    count = lax.axis_size(axis)
    spread = jnp.broadcast_to(block[None], (count,) + block.shape)
    moved = lax.all_to_all(spread, axis, 0, 0)
    return moved.reshape((count * block.shape[0],) + block.shape[1:])


def reduce_all(terms, axis):
    count = lax.axis_size(axis)
    rows = terms.shape[0] // count
    moved = lax.all_to_all(terms.astype(jnp.bfloat16).reshape((count, rows) + terms.shape[1:]), axis, 0, 0)
    return jnp.sum(moved.astype(jnp.float32), axis=0)


def normalize(inputs, gain):
    wide = inputs.astype(jnp.float32)
    inverse = lax.rsqrt(jnp.mean(wide * wide, axis=-1, keepdims=True) + EPSILON)
    return (wide * inverse * gain, wide, inverse)


INTERPRET = False


def forward_kernel(start_ref, mask_ref, query_ref, key_ref, value_ref, input_ref, out_ref, *, heads, scale):
    allowed = mask_ref[...] != 0
    window = mask_ref.shape[1]
    start = pl.multiple_of(start_ref[0], HD)
    keys = key_ref[pl.ds(start, window), :]
    values = value_ref[pl.ds(start, window), :]
    for head in range(heads):
        cols = slice(head * HD, (head + 1) * HD)
        scores = lax.dot_general(
            query_ref[:, cols], keys, (((1,), (1,)), ((), ())), preferred_element_type=jnp.float32
        ) * scale
        scores = jnp.where(allowed, scores, NEGATIVE)
        rowmax = jnp.max(scores, axis=1, keepdims=True)
        expo = jnp.where(allowed, jnp.exp(scores - rowmax), 0.0)
        total = jnp.sum(expo, axis=1, keepdims=True)
        product = jnp.dot(expo.astype(jnp.bfloat16), values, preferred_element_type=jnp.float32)
        out_ref[:, cols] = (input_ref[:, cols].astype(jnp.float32) + product / total).astype(out_ref.dtype)


def backward_kernel(start_ref, mask_ref, query_ref, key_ref, value_ref, grad_ref, dquery_ref, dkey_ref, dvalue_ref, *, heads, scale):
    allowed = mask_ref[...] != 0
    window = mask_ref.shape[1]
    start = pl.multiple_of(start_ref[0], HD)
    keys = key_ref[pl.ds(start, window), :]
    values = value_ref[pl.ds(start, window), :]
    dkey_acc = jnp.zeros((window, HD), jnp.float32)
    dvalue_acc = jnp.zeros((window, HD), jnp.float32)
    for head in range(heads):
        cols = slice(head * HD, (head + 1) * HD)
        query = query_ref[:, cols]
        grad = grad_ref[:, cols]
        scores = lax.dot_general(
            query, keys, (((1,), (1,)), ((), ())), preferred_element_type=jnp.float32
        ) * scale
        scores = jnp.where(allowed, scores, NEGATIVE)
        rowmax = jnp.max(scores, axis=1, keepdims=True)
        expo = jnp.where(allowed, jnp.exp(scores - rowmax), 0.0)
        total = jnp.sum(expo, axis=1, keepdims=True)
        probs = expo / total
        dprob = lax.dot_general(
            grad, values, (((1,), (1,)), ((), ())), preferred_element_type=jnp.float32
        )
        delta = jnp.sum(probs * dprob, axis=1, keepdims=True)
        dscore_b = (probs * (dprob - delta)).astype(jnp.bfloat16)
        probs_b = probs.astype(jnp.bfloat16)
        dquery_ref[:, cols] = jnp.dot(dscore_b, keys, preferred_element_type=jnp.float32) * scale
        dkey_acc = dkey_acc + lax.dot_general(
            dscore_b, query, (((0,), (0,)), ((), ())), preferred_element_type=jnp.float32
        )
        dvalue_acc = dvalue_acc + lax.dot_general(
            probs_b, grad, (((0,), (0,)), ((), ())), preferred_element_type=jnp.float32
        )
    dkey_ref[...] = jnp.zeros(dkey_ref.shape, dkey_ref.dtype)
    dvalue_ref[...] = jnp.zeros(dvalue_ref.shape, dvalue_ref.dtype)
    dkey_ref[pl.ds(start, window), :] = (dkey_acc * scale).astype(dkey_ref.dtype)
    dvalue_ref[pl.ds(start, window), :] = dvalue_acc.astype(dvalue_ref.dtype)


def attention_forward(start, mask, query, keys, values, inputs, group_size):
    rows, width = query.shape
    seq_len, kv_width = keys.shape
    window = mask.shape[1]
    groups = kv_width // HD
    cols = group_size * HD
    kernel = functools.partial(forward_kernel, heads=group_size, scale=HD ** (-0.5))
    return pl.pallas_call(
        kernel,
        grid=(groups,),
        in_specs=[
            pl.BlockSpec(memory_space=pltpu.SMEM),
            pl.BlockSpec((rows, window), lambda g: (0, 0)),
            pl.BlockSpec((rows, cols), lambda g: (0, g)),
            pl.BlockSpec((seq_len, HD), lambda g: (0, g)),
            pl.BlockSpec((seq_len, HD), lambda g: (0, g)),
            pl.BlockSpec((rows, cols), lambda g: (0, g)),
        ],
        out_specs=pl.BlockSpec((rows, cols), lambda g: (0, g)),
        out_shape=jax.ShapeDtypeStruct((rows, width), jnp.bfloat16),
        interpret=INTERPRET,
    )(start, mask, query, keys, values, inputs)


def attention_backward(start, mask, query, keys, values, grad, group_size):
    rows, width = query.shape
    seq_len, kv_width = keys.shape
    window = mask.shape[1]
    groups = kv_width // HD
    cols = group_size * HD
    kernel = functools.partial(backward_kernel, heads=group_size, scale=HD ** (-0.5))
    return pl.pallas_call(
        kernel,
        grid=(groups,),
        in_specs=[
            pl.BlockSpec(memory_space=pltpu.SMEM),
            pl.BlockSpec((rows, window), lambda g: (0, 0)),
            pl.BlockSpec((rows, cols), lambda g: (0, g)),
            pl.BlockSpec((seq_len, HD), lambda g: (0, g)),
            pl.BlockSpec((seq_len, HD), lambda g: (0, g)),
            pl.BlockSpec((rows, cols), lambda g: (0, g)),
        ],
        out_specs=[
            pl.BlockSpec((rows, cols), lambda g: (0, g)),
            pl.BlockSpec((seq_len, HD), lambda g: (0, g)),
            pl.BlockSpec((seq_len, HD), lambda g: (0, g)),
        ],
        out_shape=[
            jax.ShapeDtypeStruct((rows, width), jnp.float32),
            jax.ShapeDtypeStruct((seq_len, kv_width), jnp.bfloat16),
            jax.ShapeDtypeStruct((seq_len, kv_width), jnp.bfloat16),
        ],
        interpret=INTERPRET,
    )(start, mask, query, keys, values, grad)


def body(sent_fwd, sent_grad, saved_bwd, norm_gain, key_proj, value_proj, seg_fwd, seg_bwd):
    tok_rows = sent_fwd.shape[1]
    width = sent_fwd.shape[2]
    kv_width = key_proj.shape[2]
    heads = width // HD
    kv_heads = kv_width // HD
    group_size = heads // kv_heads
    scale_factor = HD ** (-0.5)
    count = lax.axis_size("ctx")
    rank = lax.axis_index("ctx")
    offset = rank * tok_rows
    query_pos = offset + jnp.arange(tok_rows, dtype=jnp.int32)
    gain = norm_gain[0]
    key_weight = key_proj[0]
    value_weight = value_proj[0]
    arrived = shifted(sent_fwd, "section", 1)[0]
    upstream = shifted(sent_grad, "section", -1)[0]

    def layer_parts(inputs):
        normed, wide, inverse = normalize(inputs, gain)
        flat = normed.astype(jnp.bfloat16)
        keys = jnp.dot(flat, key_weight, preferred_element_type=jnp.float32).astype(jnp.bfloat16)
        values = jnp.dot(flat, value_weight, preferred_element_type=jnp.float32).astype(
            jnp.bfloat16
        )
        return (flat.reshape(tok_rows, heads, HD), keys, values, wide, inverse)

    def allowed_of(segment):
        seg_query = lax.dynamic_slice_in_dim(segment, offset, tok_rows)
        key_pos = jnp.arange(segment.shape[0], dtype=jnp.int32)
        return (key_pos[None, :] <= query_pos[:, None]) & (seg_query[:, None] == segment[None, :])

    back_blocks = -(-(SEGMENT_MAX - 1) // tok_rows)
    window = min(back_blocks + 1, count) * tok_rows
    window_start = jnp.minimum(jnp.maximum(rank - back_blocks, 0) * tok_rows, count * tok_rows - window)

    bwd_query, bwd_keys, bwd_values, bwd_wide, bwd_inverse = layer_parts(saved_bwd[0])
    bwd_all = gather_all(jnp.concatenate([bwd_keys, bwd_values], axis=1), "ctx")
    fwd_query, fwd_keys, fwd_values, fwd_wide, fwd_inverse = layer_parts(arrived)
    fwd_all = gather_all(jnp.concatenate([fwd_keys, fwd_values], axis=1), "ctx")

    bwd_key_all = bwd_all[:, :kv_width]
    bwd_value_all = bwd_all[:, kv_width:]
    allowed = lax.dynamic_slice_in_dim(allowed_of(seg_bwd).astype(jnp.int32), window_start, window, axis=1)
    start_row = window_start.reshape(1).astype(jnp.int32)
    halves = 2
    fwd_halves = 1
    half_kv = kv_width // halves
    half_q = width // halves
    dquery_parts, dkey_parts, dvalue_parts = ([], [], [])
    half_terms = []
    for half in range(halves):
        kv_cols = slice(half * half_kv, (half + 1) * half_kv)
        q_cols = slice(half * half_q, (half + 1) * half_q)
        dquery_half, dkey_half, dvalue_half = attention_backward(
            start_row,
            allowed,
            bwd_query.reshape(tok_rows, width)[:, q_cols],
            bwd_key_all[:, kv_cols],
            bwd_value_all[:, kv_cols],
            upstream[:, q_cols],
            group_size,
        )
        dquery_parts.append(dquery_half)
        half_terms.append(jnp.concatenate([dkey_half, dvalue_half], axis=1))
    fwd_all, half_terms = lax.optimization_barrier((fwd_all, half_terms))

    key_piece = fwd_all[:, :kv_width]
    value_piece = fwd_all[:, kv_width:]
    allowed = lax.dynamic_slice_in_dim(allowed_of(seg_fwd).astype(jnp.int32), window_start, window, axis=1)
    dkv_all = reduce_all(jnp.concatenate(half_terms, axis=1), "ctx").astype(jnp.bfloat16)
    for half in range(halves):
        base = half * 2 * half_kv
        dkey_parts.append(dkv_all[:, base:base + half_kv])
        dvalue_parts.append(dkv_all[:, base + half_kv:base + 2 * half_kv])
    dquery = jnp.concatenate(dquery_parts, axis=1)
    dkeys = jnp.concatenate(dkey_parts, axis=1)
    dvalues = jnp.concatenate(dvalue_parts, axis=1)
    fwd_parts = []
    fwd_kv = kv_width // fwd_halves
    fwd_q = width // fwd_halves
    for half in range(fwd_halves):
        kv_cols = slice(half * fwd_kv, (half + 1) * fwd_kv)
        q_cols = slice(half * fwd_q, (half + 1) * fwd_q)
        fwd_parts.append(
            attention_forward(
                start_row,
                allowed,
                fwd_query.reshape(tok_rows, width)[:, q_cols],
                key_piece[:, kv_cols],
                value_piece[:, kv_cols],
                arrived[:, q_cols],
                group_size,
            )
        )
    fwd_out = jnp.concatenate(fwd_parts, axis=1)

    dnormed = dquery + jnp.dot(
        dkeys, jnp.transpose(key_weight), preferred_element_type=jnp.float32
    )
    dnormed = dnormed + jnp.dot(
        dvalues,
        jnp.transpose(value_weight),
        preferred_element_type=jnp.float32,
    )
    scaled = gain * dnormed
    grad_in = bwd_inverse * scaled - bwd_wide * bwd_inverse**3 * jnp.mean(
        bwd_wide * scaled, axis=-1, keepdims=True
    )
    grad_out = (upstream.astype(jnp.float32) + grad_in).astype(jnp.bfloat16)
    return (fwd_out[None], grad_out[None])


def solution(mesh):
    placed = (
        P("section", "ctx", None),
        P("section", "ctx", None),
        P("section", "ctx", None),
        P("section", None),
        P("section", None, None),
        P("section", None, None),
        P(),
        P(),
    )
    return jax.shard_map(
        body,
        mesh=mesh,
        in_specs=placed,
        out_specs=(P("section", "ctx", None), P("section", "ctx", None)),
        check_vma=False,
    )
```
